128 devices in a mesh: grp: 4 (over x), tok: 32 (over z, y, core).
Axes of the slice: x: 4, y: 4, z: 4, core: 2. Of those that a mesh axis runs over, the one named last changes fastest.
Arguments:
- tokens: bfloat16 [16384, 2560], P(('grp', 'tok')), may hold values from -6 to 6
- input_gain: bfloat16 [2560], replicated, may hold values from 0.25 to 1.75
- query_down: bfloat16 [2560, 768], replicated, may hold values from -0.125 to 0.125
- query_gain: bfloat16 [768], replicated, may hold values from 0.25 to 1.75
- query_up: bfloat16 [768, 1920], replicated, may hold values from -0.21875 to 0.21875
- latent_down: bfloat16 [2560, 288], replicated, may hold values from -0.125 to 0.125
- latent_gain: bfloat16 [256], replicated, may hold values from 0.25 to 1.75
- key_up: bfloat16 [256, 1280], replicated, may hold values from -0.375 to 0.375
- value_up: bfloat16 [256, 1280], replicated, may hold values from -0.375 to 0.375
- output_weight: bfloat16 [1280, 2560], replicated, may hold values from -0.15625 to 0.15625
- post_gain: bfloat16 [2560], replicated, may hold values from 0.25 to 1.75
- gate_weight: bfloat16 [2560, 3200], P('tok', 'grp'), may hold values from -0.125 to 0.125
- up_weight: bfloat16 [2560, 3200], P('tok', 'grp'), may hold values from -0.125 to 0.125
- down_weight: bfloat16 [3200, 2560], P('grp', 'tok'), may hold values from -0.109375 to 0.109375
- cache_latents: bfloat16 [16, 4096, 288], P('grp', 'tok'), as said below
- prompt_latents: bfloat16 [8, 1024, 288], P(None, 'tok'), as said below
- cache_len: int32 [16], replicated, may hold values from 1 to 4096, 32768 in all
- prompt_len: int32 [8], replicated, may hold values from 1 to 1024, 4096 in all
- prompt_of: int32 [16], replicated, may hold values from 0 to 7
Outputs:
- layer_out: bfloat16 [16384, 2560], P(('grp', 'tok'))
- new_latents: bfloat16 [16384, 288], P(('grp', 'tok'))
The draws below stay inside these ranges and needn't reach their ends.
Inputs may be any that keep to these rules, and one draw needn't show every extreme that they name: `cache_len`: some request has exactly 4096 live cached rows. `prompt_len`: some stored prompt has exactly 1024 live rows. `cache_latents`: rows past a request's live length are stored but never read. `prompt_latents`: rows past a prompt's live length are stored but never read.
All inputs are finite; a program needn't handle non-finite values.
Results may differ from the reference program's by a relative error of at most 0.02.
Values may be sent and summed in bfloat16 or wider, within the bound.
No kernel may reach another device: no remote copies, remote signals or barrier semaphores. Data moves between devices by JAX's collectives and lax.ppermute only.
A program may use at most 128 MiB of HBM per device.

```python
import math
import jax
import jax.numpy as jnp
import numpy as np
from jax import lax

D = 2560
QR = 768
KVR = 256
HEADS = 20
NOPE = 64
ROPE = 32
VDIM = 64
FF = 3200
SPAN = 1024
CACHE = 4096
PLEN = 1024
NPROMPT = 8
TOK_DEV = 128
REQ_GRP = 4
REQS = 16
TOKENS = 16384
N_TOK = 32


def latent_rows(key, shape):
    values = jax.random.normal(key, shape, jnp.float32)
    return values.astype(jnp.bfloat16)


def draw_cache_latents(key, part):
    return latent_rows(jax.random.fold_in(key, 11), (REQS, CACHE, KVR + ROPE))


def draw_prompt_latents(key, part):
    return latent_rows(jax.random.fold_in(key, 23), (NPROMPT, PLEN, KVR + ROPE))


def place_ends(result, stream_key, low, largest):
    spot = [jax.random.randint(jax.random.fold_in(stream_key, axis), (), 0, length) for axis, length in enumerate(result.shape)]
    longest = result.shape.index(max(result.shape))
    beside = spot[:longest] + [(spot[longest] + 1) % result.shape[longest]] + spot[longest + 1:]
    return result.at[tuple(spot)].set(low).at[tuple(beside)].set(largest)


def steps_of(key, shape, cuts, smallest, top_value):
    def one(axis_at, shards_of):
        draws = jax.random.uniform(jax.random.fold_in(jax.random.fold_in(key, 6), axis_at), (shards_of,), jnp.float32, smallest / len(cuts), top_value / len(cuts))
        return jnp.repeat(jnp.exp(draws), shape[axis_at] // shards_of).reshape((-1,) + (1,) * (len(shape) - axis_at - 1))

    level = one(*cuts[0])
    for cut in cuts[1:]:
        level = level * one(*cut)
    return level


def length_profile(amount, total, reach, slope):
    portions = [(1 << 20) // math.isqrt(grade ** slope) + 1 for grade in range(2, amount + 1)]
    spare, counts = total - reach - (amount - 1), [1] * (amount - 1)
    while spare > 0:
        free = [i for i in range(amount - 1) if counts[i] < reach]
        pool, left = sum([portions[i] for i in free]), spare
        for i in free:
            addition = min(reach - counts[i], max(1, left * portions[i] // pool), spare)
            counts[i] = counts[i] + addition
            spare = spare - addition
    return np.array([reach] + counts)


def uneven_parts(key, count, total, most, slope):
    if count == 2:
        one = jax.random.randint(key, (), max(1, total - most), min(most, total - 1) + 1)
        return jnp.stack([one, total - one])
    sizes = jnp.asarray(length_profile(count, total, most, slope), jnp.int32)
    couples = (count - 1) // 2
    source_of, sink = sizes[1:1 + 2 * couples:2], sizes[2:2 + 2 * couples:2]
    slack = jnp.minimum(source_of - 1, most - sink)
    passed = jax.random.randint(jax.random.fold_in(key, 1), (couples,), 0, 1 << 20) % (slack + 1)
    sizes = sizes.at[1:1 + 2 * couples:2].set(source_of - passed).at[2:2 + 2 * couples:2].set(sink + passed)
    return sizes[jax.random.permutation(jax.random.fold_in(key, 2), count)]


def centred(rng, extent, scale, most, pieces=(), kind=jnp.bfloat16):
    array = jax.random.normal(rng, extent, jnp.float32) * scale
    if len(pieces) > 0:
        array = steps_of(rng, extent, pieces, -0.22, 0.18) * array
    return jnp.clip(array, min=-most, max=most).astype(kind)


def setup_inputs(seed: int = 0) -> dict:
    arg_keys = jax.random.split(jax.random.key(seed), 20)
    return {
        "tokens": centred(arg_keys[0], (TOKENS, D), 1.0, 6.0, ((0, 128),)),
        "input_gain": jnp.clip(1.0 + 0.15 * jax.random.normal(arg_keys[1], (D,), jnp.float32), 0.25, 1.75).astype(jnp.bfloat16),
        "query_down": centred(arg_keys[2], (D, QR), D ** -0.5, 0.125),
        "query_gain": jnp.clip(1.0 + 0.15 * jax.random.normal(arg_keys[3], (QR,), jnp.float32), 0.25, 1.75).astype(jnp.bfloat16),
        "query_up": centred(arg_keys[4], (QR, HEADS * (NOPE + ROPE)), QR ** -0.5, 0.21875),
        "latent_down": centred(arg_keys[5], (D, KVR + ROPE), D ** -0.5, 0.125),
        "latent_gain": jnp.clip(1.0 + 0.15 * jax.random.normal(arg_keys[6], (KVR,), jnp.float32), 0.25, 1.75).astype(jnp.bfloat16),
        "key_up": centred(arg_keys[7], (KVR, HEADS * NOPE), KVR ** -0.5, 0.375),
        "value_up": centred(arg_keys[8], (KVR, HEADS * VDIM), KVR ** -0.5, 0.375),
        "output_weight": centred(arg_keys[9], (HEADS * VDIM, D), (HEADS * VDIM) ** -0.5, 0.15625),
        "post_gain": jnp.clip(1.0 + 0.15 * jax.random.normal(arg_keys[10], (D,), jnp.float32), 0.25, 1.75).astype(jnp.bfloat16),
        "gate_weight": centred(arg_keys[11], (D, FF), D ** -0.5, 0.125, ((0, 32), (1, 4))),
        "up_weight": centred(arg_keys[12], (D, FF), D ** -0.5, 0.125, ((0, 32), (1, 4))),
        "down_weight": centred(arg_keys[13], (FF, D), FF ** -0.5, 0.109375, ((0, 4), (1, 32))),
        "cache_latents": draw_cache_latents(jax.random.fold_in(arg_keys[19], 71), 0),
        "prompt_latents": draw_prompt_latents(jax.random.fold_in(arg_keys[19], 71), 0),
        "cache_len": uneven_parts(arg_keys[16], REQS, REQS * CACHE // 2, CACHE, 1).astype(jnp.int32),
        "prompt_len": uneven_parts(arg_keys[17], NPROMPT, NPROMPT * PLEN // 2, PLEN, 1).astype(jnp.int32),
        "prompt_of": place_ends(jax.random.randint(arg_keys[18], (REQS,), 0, NPROMPT), jax.random.fold_in(arg_keys[18], 1), 0, NPROMPT - 1).astype(jnp.int32),
    }


EPSILON = 1e-06

def rounded(values):
    return lax.optimization_barrier(values.astype(jnp.bfloat16))

def norm_rows(values, gain_vector):
    mean_square = lax.optimization_barrier(jnp.mean(values * values, axis=-1, keepdims=True))
    return values * lax.rsqrt(mean_square + EPSILON) * gain_vector.astype(jnp.float32)

def rotate(values, positions):
    half_width = values.shape[-1] // 2
    frequency = 10000.0 ** (-jnp.arange(half_width, dtype=jnp.float32) / half_width)
    angles = positions.astype(jnp.float32)[:, None] * frequency[None, :]
    if values.ndim == 3:
        angles = angles[:, None, :]
    cosine = jnp.cos(angles)
    sine_part = jnp.sin(angles)
    leading = values[..., :half_width]
    trailing = values[..., half_width:]
    return jnp.concatenate([leading * cosine - trailing * sine_part, trailing * cosine + leading * sine_part], axis=-1)

def reference(tokens, input_gain, query_down, query_gain, query_up, latent_down, latent_gain, key_up, value_up, output_weight, post_gain, gate_weight, up_weight, down_weight, cache_latents, prompt_latents, cache_len, prompt_len, prompt_of):
    token_count = tokens.shape[0]
    token_index = jnp.arange(token_count, dtype=jnp.int32)
    block_index_all = (token_index // TOK_DEV).astype(jnp.int32)
    row_in_block = (token_index % TOK_DEV).astype(jnp.int32)
    group_of = (block_index_all // N_TOK).astype(jnp.int32)
    shard_of = (block_index_all % N_TOK).astype(jnp.int32)
    request = (group_of * REQ_GRP + shard_of % REQ_GRP).astype(jnp.int32)
    within = (shard_of // REQ_GRP * TOK_DEV + row_in_block).astype(jnp.int32)
    sorted_index = (request * SPAN + within).astype(jnp.int32)
    slot = jnp.arange(token_count, dtype=jnp.int32)
    slot_request = (slot // SPAN).astype(jnp.int32)
    slot_place = (slot % SPAN).astype(jnp.int32)
    slot_shard = (slot_place // TOK_DEV * REQ_GRP + slot_request % REQ_GRP).astype(jnp.int32)
    order = ((slot_request // REQ_GRP * N_TOK + slot_shard) * TOK_DEV + slot_place % TOK_DEV).astype(jnp.int32)
    own_prompt = prompt_len[prompt_of].astype(jnp.int32)
    positions = (own_prompt[request] + cache_len[request] + within).astype(jnp.int32)
    normed = rounded(norm_rows(tokens.astype(jnp.float32), input_gain))
    query_latent = rounded(norm_rows(jnp.dot(normed, query_down, preferred_element_type=jnp.float32), query_gain))
    query_full = rounded(jnp.dot(query_latent, query_up, preferred_element_type=jnp.float32)).reshape(token_count, HEADS, NOPE + ROPE)
    absorbed = jnp.einsum('thd,khd->thk', query_full[..., :NOPE].astype(jnp.float32), key_up.reshape(KVR, HEADS, NOPE).astype(jnp.float32))
    turned = rotate(query_full[..., NOPE:].astype(jnp.float32), positions)
    queries = rounded(jnp.concatenate([absorbed, turned], axis=-1))
    latent_raw = jnp.dot(normed, latent_down, preferred_element_type=jnp.float32)
    new_latents = rounded(jnp.concatenate([norm_rows(latent_raw[:, :KVR], latent_gain), rotate(latent_raw[:, KVR:], positions)], axis=-1))
    queries_sorted = queries[order]
    latents_sorted = new_latents[order]
    query_block = min(256, SPAN)
    per_request = SPAN // query_block
    request_count = token_count // SPAN
    score_scale = 1.0 / (NOPE + ROPE) ** 0.5
    key_index = jnp.arange(PLEN + CACHE + SPAN, dtype=jnp.int32)

    def attend(block_index):
        owner = (block_index // per_request).astype(jnp.int32)
        first_row = (block_index % per_request * query_block).astype(jnp.int32)
        query_rows = lax.dynamic_slice_in_dim(queries_sorted, (owner * SPAN + first_row).astype(jnp.int32), query_block, 0)
        prompt_rows = lax.dynamic_index_in_dim(prompt_latents, prompt_of[owner], 0, keepdims=False)
        cache_rows = lax.dynamic_index_in_dim(cache_latents, owner, 0, keepdims=False)
        span_rows = lax.dynamic_slice_in_dim(latents_sorted, (owner * SPAN).astype(jnp.int32), SPAN, 0)
        key_rows = jnp.concatenate([prompt_rows, cache_rows, span_rows], axis=0)
        row_place = first_row + jnp.arange(query_block, dtype=jnp.int32)
        live_keys = jnp.where(key_index < PLEN, key_index < own_prompt[owner], jnp.where(key_index < PLEN + CACHE, key_index - PLEN < cache_len[owner], (key_index - PLEN - CACHE)[None, :] <= row_place[:, None]))
        live_keys = jnp.broadcast_to(live_keys, (query_block, PLEN + CACHE + SPAN))
        scores = jnp.einsum('qhw,kw->qhk', query_rows.astype(jnp.float32), key_rows.astype(jnp.float32)) * score_scale
        live_heads = live_keys[:, None, :]
        row_max = lax.optimization_barrier(jnp.max(jnp.where(live_heads, scores, -1e+30), axis=-1, keepdims=True))
        weights = jnp.where(live_heads, jnp.exp(scores - row_max), 0.0)
        row_total = lax.optimization_barrier(jnp.sum(weights, axis=-1, keepdims=True))
        mixed = jnp.einsum('qhk,kc->qhc', rounded(weights).astype(jnp.float32), key_rows[:, :KVR].astype(jnp.float32))
        return rounded(mixed / row_total)
    blocks_all = jnp.arange(request_count * per_request, dtype=jnp.int32)
    latent_sorted = lax.map(attend, blocks_all).reshape(token_count, HEADS, KVR)
    latent_out = latent_sorted[sorted_index]
    heads_out = rounded(jnp.einsum('thk,khv->thv', latent_out.astype(jnp.float32), value_up.reshape(KVR, HEADS, VDIM).astype(jnp.float32))).reshape(token_count, HEADS * VDIM)
    attended = jnp.dot(heads_out, output_weight, preferred_element_type=jnp.float32)
    residual = rounded(tokens.astype(jnp.float32) + attended)
    post_norm = rounded(norm_rows(residual.astype(jnp.float32), post_gain))
    gate_values = jnp.dot(post_norm, gate_weight, preferred_element_type=jnp.float32)
    up_values = jnp.dot(post_norm, up_weight, preferred_element_type=jnp.float32)
    hidden = rounded(jax.nn.silu(gate_values) * up_values)
    down_values = jnp.dot(hidden, down_weight, preferred_element_type=jnp.float32)
    layer_out = (residual.astype(jnp.float32) + down_values).astype(jnp.bfloat16)
    return (layer_out, new_latents)
```

```python
import jax
import jax.numpy as jnp
from jax import lax
from jax.sharding import Mesh, PartitionSpec as P

KVR = 256
HEADS = 20
NOPE = 64
ROPE = 32
VDIM = 64
SPAN = 1024


EPSILON = 1e-06


def passed_along(block, axis, distance):
    devices = range(lax.axis_size(axis))
    route = [(i - distance, i) for i in devices if i - distance in devices]
    return lax.ppermute(block, axis, route)


def norm_rows(values, gain_vector):
    mean_square = jnp.mean(values * values, axis=-1, keepdims=True)
    return values * lax.rsqrt(mean_square + EPSILON) * gain_vector.astype(jnp.float32)


def rotate(values, positions):
    half_width = values.shape[-1] // 2
    frequency = 10000.0 ** (-jnp.arange(half_width, dtype=jnp.float32) / half_width)
    angles = positions.astype(jnp.float32)[:, None] * frequency[None, :]
    if values.ndim == 3:
        angles = angles[:, None, :]
    cosine = jnp.cos(angles)
    sine_part = jnp.sin(angles)
    leading = values[..., :half_width]
    trailing = values[..., half_width:]
    return jnp.concatenate(
        [leading * cosine - trailing * sine_part, trailing * cosine + leading * sine_part], axis=-1
    )


def attend_segment(
    softmax_state, queries, key_rows, lowers, limits, block_count, key_block, score_scale
):

    def fold_block(step_index, carried):
        running_max, running_sum, running_out = carried
        first_key = step_index * key_block
        key_piece = lax.dynamic_slice_in_dim(key_rows, first_key, key_block, 0)
        scores = (
            jnp.einsum("rw,kw->rk", queries, key_piece, preferred_element_type=jnp.float32)
            * score_scale
        )
        key_place = (first_key + jnp.arange(key_block, dtype=jnp.int32))[None, :]
        live_keys = jnp.logical_and(key_place >= lowers[:, None], key_place < limits[:, None])
        next_max = jnp.maximum(running_max, jnp.max(jnp.where(live_keys, scores, -1e30), axis=1))
        weights = jnp.where(live_keys, jnp.exp(scores - next_max[:, None]), 0.0)
        factor = jnp.exp(running_max - next_max)
        running_sum = running_sum * factor + jnp.sum(weights, axis=1)
        running_out = running_out * factor[:, None] + jnp.dot(
            weights.astype(jnp.bfloat16), key_piece[:, :KVR], preferred_element_type=jnp.float32
        )
        return (next_max, running_sum, running_out)

    return lax.fori_loop(0, block_count, fold_block, softmax_state)


def body(
    tokens,
    input_gain,
    query_down,
    query_gain,
    query_up,
    latent_down,
    latent_gain,
    key_up,
    value_up,
    output_weight,
    post_gain,
    gate_weight,
    up_weight,
    down_weight,
    cache_latents,
    prompt_latents,
    cache_len,
    prompt_len,
    prompt_of,
):
    group_index = lax.axis_index("grp")
    span_index = lax.axis_index("tq")
    local_request = lax.axis_index("tr")
    tok_dev = tokens.shape[0]
    group_requests = lax.axis_size("tr")
    owner = group_index * group_requests + local_request
    offset = span_index * tok_dev
    within = offset + jnp.arange(tok_dev, dtype=jnp.int32)
    own_prompt = prompt_of[owner]
    prompt_live = prompt_len[own_prompt]
    cache_live = cache_len[owner]
    positions = prompt_live + cache_live + within
    normed = norm_rows(tokens.astype(jnp.float32), input_gain).astype(jnp.bfloat16)
    query_latent = norm_rows(
        jnp.dot(normed, query_down, preferred_element_type=jnp.float32), query_gain
    ).astype(jnp.bfloat16)
    query_full = jnp.dot(query_latent, query_up, preferred_element_type=jnp.float32).astype(
        jnp.bfloat16
    )
    query_full = lax.optimization_barrier(query_full).reshape(tok_dev, HEADS, NOPE + ROPE)
    absorbed = jnp.einsum(
        "thd,khd->thk",
        query_full[..., :NOPE],
        key_up.reshape(KVR, HEADS, NOPE),
        preferred_element_type=jnp.float32,
    )
    turned = rotate(query_full[..., NOPE:].astype(jnp.float32), positions)
    queries = jnp.concatenate([absorbed, turned], axis=-1).astype(jnp.bfloat16)
    latent_raw = jnp.dot(normed, latent_down, preferred_element_type=jnp.float32)
    new_latents = jnp.concatenate(
        [norm_rows(latent_raw[:, :KVR], latent_gain), rotate(latent_raw[:, KVR:], positions)],
        axis=-1,
    ).astype(jnp.bfloat16)
    latent_width = new_latents.shape[1]
    span_rows = lax.all_gather(new_latents, "tq", axis=0, tiled=True)
    span_lower = jnp.zeros((tok_dev,), jnp.int32)
    span_limit = within + 1
    cache_mine = lax.all_to_all(cache_latents, "tr", 0, 1, tiled=True)
    group_prompts = prompt_of[group_index * group_requests + jnp.arange(group_requests)]
    prompt_send = jnp.take(prompt_latents, group_prompts, axis=0)
    prompt_mine = lax.all_to_all(prompt_send, "tr", 0, 1, tiled=True)
    prompt_piece = prompt_mine.shape[1]
    key_pieces = lax.all_gather(
        jnp.concatenate([prompt_mine, cache_mine], axis=1)[0], "tq", axis=0
    )
    prompt_rows = key_pieces[:, :prompt_piece].reshape(-1, latent_width)
    cache_rows = key_pieces[:, prompt_piece:].reshape(-1, latent_width)
    query_rows = queries.reshape(tok_dev * HEADS, latent_width)
    row_count = tok_dev * HEADS
    score_scale = 1.0 / (NOPE + ROPE) ** 0.5
    softmax_state = (
        jnp.full((row_count,), -1e30, jnp.float32),
        jnp.zeros((row_count,), jnp.float32),
        jnp.zeros((row_count, KVR), jnp.float32),
    )
    no_lower = jnp.zeros((tok_dev,), jnp.int32)
    segments = (
        (span_rows, span_lower, span_limit),
        (prompt_rows, no_lower, jnp.broadcast_to(prompt_live, (tok_dev,))),
        (cache_rows, no_lower, jnp.broadcast_to(cache_live, (tok_dev,))),
    )
    for key_rows, token_lower, token_limit in segments:
        lowers = jnp.repeat(token_lower, HEADS)
        limits = jnp.repeat(token_limit, HEADS)
        key_block = min(512, key_rows.shape[0])
        block_count = key_rows.shape[0] // key_block
        softmax_state = attend_segment(
            softmax_state, query_rows, key_rows, lowers, limits, block_count, key_block, score_scale
        )
    running_max, running_sum, running_out = softmax_state
    latent_out = (
        (running_out / running_sum[:, None]).astype(jnp.bfloat16).reshape(tok_dev, HEADS, KVR)
    )
    heads_out = (
        jnp.einsum(
            "thk,khv->thv",
            latent_out,
            value_up.reshape(KVR, HEADS, VDIM),
            preferred_element_type=jnp.float32,
        )
        .astype(jnp.bfloat16)
        .reshape(tok_dev, HEADS * VDIM)
    )
    attended = jnp.dot(heads_out, output_weight, preferred_element_type=jnp.float32)
    weights_full = lax.all_gather(
        jnp.stack([gate_weight, up_weight, down_weight.T]), ("tq", "tr"), axis=1, tiled=True
    )
    residual, weights_full = lax.optimization_barrier(
        ((tokens.astype(jnp.float32) + attended).astype(jnp.bfloat16), weights_full)
    )
    post_norm = norm_rows(residual.astype(jnp.float32), post_gain).astype(jnp.bfloat16)
    rows_all = lax.all_gather(post_norm, "grp", axis=0, tiled=True)
    gate_full, up_full, down_full = weights_full
    gate_values = jnp.dot(rows_all, gate_full, preferred_element_type=jnp.float32)
    up_values = jnp.dot(rows_all, up_full, preferred_element_type=jnp.float32)
    hidden = (jax.nn.silu(gate_values) * up_values).astype(jnp.bfloat16)
    partial_out = lax.dot_general(
        hidden, down_full, (((1,), (1,)), ((), ())), preferred_element_type=jnp.float32
    )
    down_values = lax.psum_scatter(
        partial_out.astype(jnp.bfloat16), "grp", scatter_dimension=0, tiled=True
    ).astype(jnp.float32)
    layer_out = (residual.astype(jnp.float32) + down_values).astype(jnp.bfloat16)
    return (layer_out, new_latents)


def solution(mesh):
    split = ("grp", "tq", "tr")
    tokens_spec = P(split, None)
    in_specs = (
        tokens_spec,
        P(),
        P(),
        P(),
        P(),
        P(),
        P(),
        P(),
        P(),
        P(),
        P(),
        P(("tq", "tr"), "grp"),
        P(("tq", "tr"), "grp"),
        P("grp", ("tq", "tr")),
        P("grp", ("tq", "tr"), None),
        P(None, ("tq", "tr"), None),
        P(),
        P(),
        P(),
    )
    out_specs = (tokens_spec, tokens_spec)

    def run(*args):
        n_grp, n_tok = mesh.shape["grp"], mesh.shape["tok"]
        tok_dev = args[0].shape[0] // (n_grp * n_tok)
        group_requests = tok_dev * n_tok // SPAN
        sub = Mesh(
            mesh.devices.reshape(n_grp, n_tok // group_requests, group_requests), split
        )
        return jax.shard_map(
            body, mesh=sub, in_specs=in_specs, out_specs=out_specs, check_vma=False
        )(*args)

    return run
```

```python
import jax
import jax.numpy as jnp
from jax import lax
from jax.sharding import Mesh, PartitionSpec as P

KVR = 256
HEADS = 20
NOPE = 64
ROPE = 32
VDIM = 64
SPAN = 1024
FFN_CHUNKS = 2


EPSILON = 1e-06


def passed_along(block, axis, distance):
    devices = range(lax.axis_size(axis))
    route = [(i - distance, i) for i in devices if i - distance in devices]
    return lax.ppermute(block, axis, route)


def norm_rows(values, gain_vector):
    mean_square = jnp.mean(values * values, axis=-1, keepdims=True)
    return values * lax.rsqrt(mean_square + EPSILON) * gain_vector.astype(jnp.float32)


def rotate(values, positions):
    half_width = values.shape[-1] // 2
    frequency = 10000.0 ** (-jnp.arange(half_width, dtype=jnp.float32) / half_width)
    angles = positions.astype(jnp.float32)[:, None] * frequency[None, :]
    if values.ndim == 3:
        angles = angles[:, None, :]
    cosine = jnp.cos(angles)
    sine_part = jnp.sin(angles)
    leading = values[..., :half_width]
    trailing = values[..., half_width:]
    return jnp.concatenate(
        [leading * cosine - trailing * sine_part, trailing * cosine + leading * sine_part], axis=-1
    )


def attend_segment(
    softmax_state, queries, key_rows, lowers, limits, block_count, key_block, score_scale
):

    def fold_block(step_index, carried):
        running_max, running_sum, running_out = carried
        first_key = step_index * key_block
        key_piece = lax.dynamic_slice_in_dim(key_rows, first_key, key_block, 0)
        scores = (
            jnp.einsum("rw,kw->rk", queries, key_piece, preferred_element_type=jnp.float32)
            * score_scale
        )
        key_place = (first_key + jnp.arange(key_block, dtype=jnp.int32))[None, :]
        live_keys = jnp.logical_and(key_place >= lowers[:, None], key_place < limits[:, None])
        next_max = jnp.maximum(running_max, jnp.max(jnp.where(live_keys, scores, -1e30), axis=1))
        weights = jnp.where(live_keys, jnp.exp(scores - next_max[:, None]), 0.0)
        factor = jnp.exp(running_max - next_max)
        running_sum = running_sum * factor + jnp.sum(weights, axis=1)
        running_out = running_out * factor[:, None] + jnp.dot(
            weights.astype(jnp.bfloat16), key_piece[:, :KVR], preferred_element_type=jnp.float32
        )
        return (next_max, running_sum, running_out)

    return lax.fori_loop(0, block_count, fold_block, softmax_state)


def body(
    tokens,
    input_gain,
    query_down,
    query_gain,
    query_up,
    latent_down,
    latent_gain,
    key_up,
    value_up,
    output_weight,
    post_gain,
    gate_weight,
    up_weight,
    down_weight,
    cache_latents,
    prompt_latents,
    cache_len,
    prompt_len,
    prompt_of,
):
    group_index = lax.axis_index("grp")
    span_index = lax.axis_index("tq")
    local_request = lax.axis_index("tr")
    tok_dev = tokens.shape[0]
    group_requests = lax.axis_size("tr")
    owner = group_index * group_requests + local_request
    offset = span_index * tok_dev
    within = offset + jnp.arange(tok_dev, dtype=jnp.int32)
    own_prompt = prompt_of[owner]
    prompt_live = prompt_len[own_prompt]
    cache_live = cache_len[owner]
    positions = prompt_live + cache_live + within
    normed = norm_rows(tokens.astype(jnp.float32), input_gain).astype(jnp.bfloat16)
    query_latent = norm_rows(
        jnp.dot(normed, query_down, preferred_element_type=jnp.float32), query_gain
    ).astype(jnp.bfloat16)
    query_full = jnp.dot(query_latent, query_up, preferred_element_type=jnp.float32).astype(
        jnp.bfloat16
    )
    query_full = lax.optimization_barrier(query_full).reshape(tok_dev, HEADS, NOPE + ROPE)
    absorbed = jnp.einsum(
        "thd,khd->thk",
        query_full[..., :NOPE],
        key_up.reshape(KVR, HEADS, NOPE),
        preferred_element_type=jnp.float32,
    )
    turned = rotate(query_full[..., NOPE:].astype(jnp.float32), positions)
    queries = jnp.concatenate([absorbed, turned], axis=-1).astype(jnp.bfloat16)
    latent_raw = jnp.dot(normed, latent_down, preferred_element_type=jnp.float32)
    new_latents = jnp.concatenate(
        [norm_rows(latent_raw[:, :KVR], latent_gain), rotate(latent_raw[:, KVR:], positions)],
        axis=-1,
    ).astype(jnp.bfloat16)
    latent_width = new_latents.shape[1]
    span_lower = jnp.zeros((tok_dev,), jnp.int32)
    span_limit = within + 1
    cache_mine = lax.all_to_all(cache_latents, "tr", 0, 1, tiled=True)
    group_prompts = prompt_of[group_index * group_requests + jnp.arange(group_requests)]
    prompt_send = jnp.take(prompt_latents, group_prompts, axis=0)
    prompt_mine = lax.all_to_all(prompt_send, "tr", 0, 1, tiled=True)
    prompt_piece = prompt_mine.shape[1]
    cache_piece = cache_mine.shape[1]
    key_pieces = lax.all_gather(
        jnp.concatenate([prompt_mine[0], cache_mine[0], new_latents], axis=0), "tq", axis=0
    )
    prompt_rows = key_pieces[:, :prompt_piece].reshape(-1, latent_width)
    cache_rows = key_pieces[:, prompt_piece : prompt_piece + cache_piece].reshape(-1, latent_width)
    span_rows = key_pieces[:, prompt_piece + cache_piece :].reshape(-1, latent_width)
    query_rows = queries.reshape(tok_dev * HEADS, latent_width)
    row_count = tok_dev * HEADS
    score_scale = 1.0 / (NOPE + ROPE) ** 0.5
    softmax_state = (
        jnp.full((row_count,), -1e30, jnp.float32),
        jnp.zeros((row_count,), jnp.float32),
        jnp.zeros((row_count, KVR), jnp.float32),
    )
    no_lower = jnp.zeros((tok_dev,), jnp.int32)
    segments = (
        (span_rows, span_lower, span_limit),
        (prompt_rows, no_lower, jnp.broadcast_to(prompt_live, (tok_dev,))),
        (cache_rows, no_lower, jnp.broadcast_to(cache_live, (tok_dev,))),
    )
    for key_rows, token_lower, token_limit in segments:
        lowers = jnp.repeat(token_lower, HEADS)
        limits = jnp.repeat(token_limit, HEADS)
        key_block = min(512, key_rows.shape[0])
        block_count = key_rows.shape[0] // key_block
        softmax_state = attend_segment(
            softmax_state, query_rows, key_rows, lowers, limits, block_count, key_block, score_scale
        )
    running_max, running_sum, running_out = softmax_state
    latent_out = (
        (running_out / running_sum[:, None]).astype(jnp.bfloat16).reshape(tok_dev, HEADS, KVR)
    )
    heads_out = (
        jnp.einsum(
            "thk,khv->thv",
            latent_out,
            value_up.reshape(KVR, HEADS, VDIM),
            preferred_element_type=jnp.float32,
        )
        .astype(jnp.bfloat16)
        .reshape(tok_dev, HEADS * VDIM)
    )
    attended = jnp.dot(heads_out, output_weight, preferred_element_type=jnp.float32)
    weights_full = lax.all_gather(
        jnp.stack([gate_weight, up_weight, down_weight.T]), ("tq", "tr"), axis=1, tiled=True
    )
    residual, weights_full = lax.optimization_barrier(
        ((tokens.astype(jnp.float32) + attended).astype(jnp.bfloat16), weights_full)
    )
    post_norm = norm_rows(residual.astype(jnp.float32), post_gain).astype(jnp.bfloat16)
    gate_full, up_full, down_full = weights_full
    chunk_rows = tok_dev // FFN_CHUNKS
    down_parts = []
    for chunk in range(FFN_CHUNKS):
        rows_all = lax.all_gather(
            post_norm[chunk * chunk_rows : (chunk + 1) * chunk_rows], "grp", axis=0, tiled=True
        )
        gate_values = jnp.dot(rows_all, gate_full, preferred_element_type=jnp.float32)
        up_values = jnp.dot(rows_all, up_full, preferred_element_type=jnp.float32)
        hidden = (jax.nn.silu(gate_values) * up_values).astype(jnp.bfloat16)
        partial_out = lax.dot_general(
            hidden, down_full, (((1,), (1,)), ((), ())), preferred_element_type=jnp.float32
        )
        down_parts.append(
            lax.psum_scatter(
                partial_out.astype(jnp.bfloat16), "grp", scatter_dimension=0, tiled=True
            )
        )
    down_values = jnp.concatenate(down_parts, axis=0).astype(jnp.float32)
    layer_out = (residual.astype(jnp.float32) + down_values).astype(jnp.bfloat16)
    return (layer_out, new_latents)


def solution(mesh):
    split = ("grp", "tq", "tr")
    tokens_spec = P(split, None)
    in_specs = (
        tokens_spec,
        P(),
        P(),
        P(),
        P(),
        P(),
        P(),
        P(),
        P(),
        P(),
        P(),
        P(("tq", "tr"), "grp"),
        P(("tq", "tr"), "grp"),
        P("grp", ("tq", "tr")),
        P("grp", ("tq", "tr"), None),
        P(None, ("tq", "tr"), None),
        P(),
        P(),
        P(),
    )
    out_specs = (tokens_spec, tokens_spec)

    def run(*args):
        n_grp, n_tok = mesh.shape["grp"], mesh.shape["tok"]
        tok_dev = args[0].shape[0] // (n_grp * n_tok)
        group_requests = tok_dev * n_tok // SPAN
        sub = Mesh(
            mesh.devices.reshape(n_grp, n_tok // group_requests, group_requests), split
        )
        return jax.shard_map(
            body, mesh=sub, in_specs=in_specs, out_specs=out_specs, check_vma=False
        )(*args)

    return run
```

```python
import jax
import jax.numpy as jnp
from jax import lax
from jax.sharding import Mesh, PartitionSpec as P

KVR = 256
HEADS = 20
NOPE = 64
ROPE = 32
VDIM = 64
SPAN = 1024


EPSILON = 1e-06


def passed_along(block, axis, distance):
    devices = range(lax.axis_size(axis))
    route = [(i - distance, i) for i in devices if i - distance in devices]
    return lax.ppermute(block, axis, route)


def norm_rows(values, gain_vector):
    mean_square = jnp.mean(values * values, axis=-1, keepdims=True)
    return values * lax.rsqrt(mean_square + EPSILON) * gain_vector.astype(jnp.float32)


def rotate(values, positions):
    half_width = values.shape[-1] // 2
    frequency = 10000.0 ** (-jnp.arange(half_width, dtype=jnp.float32) / half_width)
    angles = positions.astype(jnp.float32)[:, None] * frequency[None, :]
    if values.ndim == 3:
        angles = angles[:, None, :]
    cosine = jnp.cos(angles)
    sine_part = jnp.sin(angles)
    leading = values[..., :half_width]
    trailing = values[..., half_width:]
    return jnp.concatenate(
        [leading * cosine - trailing * sine_part, trailing * cosine + leading * sine_part], axis=-1
    )


def attend_segment(
    softmax_state, queries, key_rows, lowers, limits, block_count, key_block, score_scale
):

    def fold_block(step_index, carried):
        running_max, running_sum, running_out = carried
        first_key = step_index * key_block
        key_piece = lax.dynamic_slice_in_dim(key_rows, first_key, key_block, 0)
        scores = (
            jnp.einsum("rw,kw->rk", queries, key_piece, preferred_element_type=jnp.float32)
            * score_scale
        )
        key_place = (first_key + jnp.arange(key_block, dtype=jnp.int32))[None, :]
        live_keys = jnp.logical_and(key_place >= lowers[:, None], key_place < limits[:, None])
        next_max = jnp.maximum(running_max, jnp.max(jnp.where(live_keys, scores, -1e30), axis=1))
        weights = jnp.where(live_keys, jnp.exp(scores - next_max[:, None]), 0.0)
        factor = jnp.exp(running_max - next_max)
        running_sum = running_sum * factor + jnp.sum(weights, axis=1)
        running_out = running_out * factor[:, None] + jnp.dot(
            weights.astype(jnp.bfloat16), key_piece[:, :KVR], preferred_element_type=jnp.float32
        )
        return (next_max, running_sum, running_out)

    return lax.fori_loop(0, block_count, fold_block, softmax_state)


def body(
    tokens,
    input_gain,
    query_down,
    query_gain,
    query_up,
    latent_down,
    latent_gain,
    key_up,
    value_up,
    output_weight,
    post_gain,
    gate_weight,
    up_weight,
    down_weight,
    cache_latents,
    prompt_latents,
    cache_len,
    prompt_len,
    prompt_of,
):
    group_index = lax.axis_index("grp")
    span_index = lax.axis_index("tq")
    local_request = lax.axis_index("tr")
    tok_dev = tokens.shape[0]
    group_requests = lax.axis_size("tr")
    owner = group_index * group_requests + local_request
    offset = span_index * tok_dev
    within = offset + jnp.arange(tok_dev, dtype=jnp.int32)
    own_prompt = prompt_of[owner]
    prompt_live = prompt_len[own_prompt]
    cache_live = cache_len[owner]
    positions = prompt_live + cache_live + within
    normed = norm_rows(tokens.astype(jnp.float32), input_gain).astype(jnp.bfloat16)
    query_latent = norm_rows(
        jnp.dot(normed, query_down, preferred_element_type=jnp.float32), query_gain
    ).astype(jnp.bfloat16)
    query_full = jnp.dot(query_latent, query_up, preferred_element_type=jnp.float32).astype(
        jnp.bfloat16
    )
    query_full = lax.optimization_barrier(query_full).reshape(tok_dev, HEADS, NOPE + ROPE)
    absorbed = jnp.einsum(
        "thd,khd->thk",
        query_full[..., :NOPE],
        key_up.reshape(KVR, HEADS, NOPE),
        preferred_element_type=jnp.float32,
    )
    turned = rotate(query_full[..., NOPE:].astype(jnp.float32), positions)
    queries = jnp.concatenate([absorbed, turned], axis=-1).astype(jnp.bfloat16)
    latent_raw = jnp.dot(normed, latent_down, preferred_element_type=jnp.float32)
    new_latents = jnp.concatenate(
        [norm_rows(latent_raw[:, :KVR], latent_gain), rotate(latent_raw[:, KVR:], positions)],
        axis=-1,
    ).astype(jnp.bfloat16)
    latent_width = new_latents.shape[1]
    span_blocks = lax.axis_size("tq")
    span_rows = lax.all_to_all(
        jnp.broadcast_to(new_latents, (span_blocks,) + new_latents.shape), "tq", 0, 0, tiled=True
    ).reshape(-1, latent_width)
    span_lower = jnp.zeros((tok_dev,), jnp.int32)
    span_limit = within + 1
    cache_rows = lax.all_to_all(
        jnp.tile(cache_latents, (span_blocks, 1, 1)), ("tq", "tr"), 0, 0, tiled=True
    ).reshape(-1, latent_width)
    group_prompts = prompt_of[group_index * group_requests + jnp.arange(group_requests)]
    prompt_send = jnp.take(prompt_latents, group_prompts, axis=0)
    prompt_rows = lax.all_to_all(
        jnp.tile(prompt_send, (span_blocks, 1, 1)), ("tq", "tr"), 0, 0, tiled=True
    ).reshape(-1, latent_width)
    query_rows = queries.reshape(tok_dev * HEADS, latent_width)
    row_count = tok_dev * HEADS
    score_scale = 1.0 / (NOPE + ROPE) ** 0.5
    softmax_state = (
        jnp.full((row_count,), -1e30, jnp.float32),
        jnp.zeros((row_count,), jnp.float32),
        jnp.zeros((row_count, KVR), jnp.float32),
    )
    no_lower = jnp.zeros((tok_dev,), jnp.int32)
    segments = (
        (prompt_rows, no_lower, jnp.broadcast_to(prompt_live, (tok_dev,))),
        (cache_rows, no_lower, jnp.broadcast_to(cache_live, (tok_dev,))),
        (span_rows, span_lower, span_limit),
    )
    for key_rows, token_lower, token_limit in segments:
        lowers = jnp.repeat(token_lower, HEADS)
        limits = jnp.repeat(token_limit, HEADS)
        key_block = min(512, key_rows.shape[0])
        block_count = key_rows.shape[0] // key_block
        softmax_state = attend_segment(
            softmax_state, query_rows, key_rows, lowers, limits, block_count, key_block, score_scale
        )
    running_max, running_sum, running_out = softmax_state
    latent_out = (
        (running_out / running_sum[:, None]).astype(jnp.bfloat16).reshape(tok_dev, HEADS, KVR)
    )
    heads_out = (
        jnp.einsum(
            "thk,khv->thv",
            latent_out,
            value_up.reshape(KVR, HEADS, VDIM),
            preferred_element_type=jnp.float32,
        )
        .astype(jnp.bfloat16)
        .reshape(tok_dev, HEADS * VDIM)
    )
    attended = jnp.dot(heads_out, output_weight, preferred_element_type=jnp.float32)
    weights_full = lax.all_gather(
        jnp.stack([gate_weight, up_weight, down_weight.T]), ("tq", "tr"), axis=1, tiled=True
    )
    residual, weights_full = lax.optimization_barrier(
        ((tokens.astype(jnp.float32) + attended).astype(jnp.bfloat16), weights_full)
    )
    post_norm = norm_rows(residual.astype(jnp.float32), post_gain).astype(jnp.bfloat16)
    rows_all = lax.all_gather(post_norm, "grp", axis=0, tiled=True)
    gate_full, up_full, down_full = weights_full
    gate_values = jnp.dot(rows_all, gate_full, preferred_element_type=jnp.float32)
    up_values = jnp.dot(rows_all, up_full, preferred_element_type=jnp.float32)
    hidden = (jax.nn.silu(gate_values) * up_values).astype(jnp.bfloat16)
    partial_out = lax.dot_general(
        hidden, down_full, (((1,), (1,)), ((), ())), preferred_element_type=jnp.float32
    )
    down_values = lax.psum_scatter(
        partial_out.astype(jnp.bfloat16), "grp", scatter_dimension=0, tiled=True
    ).astype(jnp.float32)
    layer_out = (residual.astype(jnp.float32) + down_values).astype(jnp.bfloat16)
    return (layer_out, new_latents)


def solution(mesh):
    split = ("grp", "tq", "tr")
    tokens_spec = P(split, None)
    in_specs = (
        tokens_spec,
        P(),
        P(),
        P(),
        P(),
        P(),
        P(),
        P(),
        P(),
        P(),
        P(),
        P(("tq", "tr"), "grp"),
        P(("tq", "tr"), "grp"),
        P("grp", ("tq", "tr")),
        P("grp", ("tq", "tr"), None),
        P(None, ("tq", "tr"), None),
        P(),
        P(),
        P(),
    )
    out_specs = (tokens_spec, tokens_spec)

    def run(*args):
        n_grp, n_tok = mesh.shape["grp"], mesh.shape["tok"]
        tok_dev = args[0].shape[0] // (n_grp * n_tok)
        group_requests = tok_dev * n_tok // SPAN
        sub = Mesh(
            mesh.devices.reshape(n_grp, n_tok // group_requests, group_requests), split
        )
        return jax.shard_map(
            body, mesh=sub, in_specs=in_specs, out_specs=out_specs, check_vma=False
        )(*args)

    return run
```

```python
import jax
import jax.numpy as jnp
from jax import lax
from jax.sharding import Mesh, PartitionSpec as P
import functools
from jax.experimental import pallas as pl
from jax.experimental.pallas import tpu as pltpu

KVR = 256
HEADS = 20
NOPE = 64
ROPE = 32
VDIM = 64
SPAN = 1024


EPSILON = 1e-06


def passed_along(block, axis, distance):
    devices = range(lax.axis_size(axis))
    route = [(i - distance, i) for i in devices if i - distance in devices]
    return lax.ppermute(block, axis, route)


def norm_rows(values, gain_vector):
    mean_square = jnp.mean(values * values, axis=-1, keepdims=True)
    return values * lax.rsqrt(mean_square + EPSILON) * gain_vector.astype(jnp.float32)


def rotate(values, positions):
    half_width = values.shape[-1] // 2
    frequency = 10000.0 ** (-jnp.arange(half_width, dtype=jnp.float32) / half_width)
    angles = positions.astype(jnp.float32)[:, None] * frequency[None, :]
    if values.ndim == 3:
        angles = angles[:, None, :]
    cosine = jnp.cos(angles)
    sine_part = jnp.sin(angles)
    leading = values[..., :half_width]
    trailing = values[..., half_width:]
    return jnp.concatenate(
        [leading * cosine - trailing * sine_part, trailing * cosine + leading * sine_part], axis=-1
    )


KEY_BLOCK = 1024
ROW_BLOCK = 640


def flash_kernel(lims_ref, lim_row_ref, q_ref, kp_ref, kc_ref, ks_ref, o_ref, m_sc, l_sc, acc_sc, *, cache_blocks, score_scale, value_width):
    j = pl.program_id(1)
    last = cache_blocks + 1

    @pl.when(j == 0)
    def _init():
        m_sc[...] = jnp.full(m_sc.shape, -1e30, jnp.float32)
        l_sc[...] = jnp.zeros(l_sc.shape, jnp.float32)
        acc_sc[...] = jnp.zeros(acc_sc.shape, jnp.float32)

    def step(k_ref, base, limit):
        keys = k_ref[...]
        scores = lax.dot_general(q_ref[...], keys, (((1,), (1,)), ((), ())), preferred_element_type=jnp.float32) * score_scale
        place = lax.broadcasted_iota(jnp.int32, scores.shape, 1) + base
        live = place < limit
        m_old = m_sc[...]
        m_new = jnp.maximum(m_old, jnp.max(jnp.where(live, scores, -1e30), axis=1, keepdims=True))
        weights = jnp.where(live, jnp.exp(scores - m_new), 0.0)
        factor = jnp.exp(m_old - m_new)
        l_sc[...] = l_sc[...] * factor + jnp.sum(weights, axis=1, keepdims=True)
        acc_sc[...] = acc_sc[...] * factor + jnp.dot(weights.astype(jnp.bfloat16), keys[:, :value_width], preferred_element_type=jnp.float32)
        m_sc[...] = m_new

    rows = q_ref.shape[0]

    @pl.when(j == 0)
    def _prompt():
        step(kp_ref, 0, jnp.full((rows, 1), lims_ref[0], jnp.int32))

    @pl.when(jnp.logical_and(j >= 1, j < last))
    def _cache():
        step(kc_ref, (j - 1) * KEY_BLOCK, jnp.full((rows, 1), lims_ref[1], jnp.int32))

    @pl.when(j == last)
    def _span():
        step(ks_ref, 0, lim_row_ref[...])
        o_ref[...] = (acc_sc[...] / l_sc[...]).astype(o_ref.dtype)


def flash_attend(lims, lim_rows, queries, prompt_rows, cache_rows, span_rows, score_scale, value_width, interpret=False):
    row_count, width = queries.shape
    cache_blocks = cache_rows.shape[0] // KEY_BLOCK
    assert prompt_rows.shape[0] == KEY_BLOCK and span_rows.shape[0] == KEY_BLOCK
    assert cache_blocks * KEY_BLOCK == cache_rows.shape[0] and row_count % ROW_BLOCK == 0
    grid = (row_count // ROW_BLOCK, cache_blocks + 2)
    key_spec = pl.BlockSpec((KEY_BLOCK, width), lambda i, j, lims: (0, 0))
    cache_spec = pl.BlockSpec((KEY_BLOCK, width), lambda i, j, lims: (jnp.minimum(jnp.maximum(j - 1, 0), cache_blocks - 1), 0))
    kernel = functools.partial(flash_kernel, cache_blocks=cache_blocks, score_scale=score_scale, value_width=value_width)
    return pl.pallas_call(
        kernel,
        grid_spec=pltpu.PrefetchScalarGridSpec(
            num_scalar_prefetch=1,
            grid=grid,
            in_specs=[
                pl.BlockSpec((ROW_BLOCK, 1), lambda i, j, lims: (i, 0)),
                pl.BlockSpec((ROW_BLOCK, width), lambda i, j, lims: (i, 0)),
                key_spec,
                cache_spec,
                key_spec,
            ],
            out_specs=pl.BlockSpec((ROW_BLOCK, value_width), lambda i, j, lims: (i, 0)),
            scratch_shapes=[
                pltpu.VMEM((ROW_BLOCK, 1), jnp.float32),
                pltpu.VMEM((ROW_BLOCK, 1), jnp.float32),
                pltpu.VMEM((ROW_BLOCK, value_width), jnp.float32),
            ],
        ),
        out_shape=jax.ShapeDtypeStruct((row_count, value_width), jnp.bfloat16),
        compiler_params=pltpu.CompilerParams(dimension_semantics=("arbitrary", "arbitrary")),
        interpret=interpret,
    )(lims, lim_rows, queries, prompt_rows, cache_rows, span_rows)


def attend_segment(
    softmax_state, queries, key_rows, lowers, limits, block_count, key_block, score_scale
):

    def fold_block(step_index, carried):
        running_max, running_sum, running_out = carried
        first_key = step_index * key_block
        key_piece = lax.dynamic_slice_in_dim(key_rows, first_key, key_block, 0)
        scores = (
            jnp.einsum("rw,kw->rk", queries, key_piece, preferred_element_type=jnp.float32)
            * score_scale
        )
        key_place = (first_key + jnp.arange(key_block, dtype=jnp.int32))[None, :]
        live_keys = jnp.logical_and(key_place >= lowers[:, None], key_place < limits[:, None])
        next_max = jnp.maximum(running_max, jnp.max(jnp.where(live_keys, scores, -1e30), axis=1))
        weights = jnp.where(live_keys, jnp.exp(scores - next_max[:, None]), 0.0)
        factor = jnp.exp(running_max - next_max)
        running_sum = running_sum * factor + jnp.sum(weights, axis=1)
        running_out = running_out * factor[:, None] + jnp.dot(
            weights.astype(jnp.bfloat16), key_piece[:, :KVR], preferred_element_type=jnp.float32
        )
        return (next_max, running_sum, running_out)

    return lax.fori_loop(0, block_count, fold_block, softmax_state)


def body(
    tokens,
    input_gain,
    query_down,
    query_gain,
    query_up,
    latent_down,
    latent_gain,
    key_up,
    value_up,
    output_weight,
    post_gain,
    gate_weight,
    up_weight,
    down_weight,
    cache_latents,
    prompt_latents,
    cache_len,
    prompt_len,
    prompt_of,
):
    group_index = lax.axis_index("grp")
    span_index = lax.axis_index("tq")
    local_request = lax.axis_index("tr")
    tok_dev = tokens.shape[0]
    group_requests = lax.axis_size("tr")
    owner = group_index * group_requests + local_request
    offset = span_index * tok_dev
    within = offset + jnp.arange(tok_dev, dtype=jnp.int32)
    own_prompt = prompt_of[owner]
    prompt_live = prompt_len[own_prompt]
    cache_live = cache_len[owner]
    positions = prompt_live + cache_live + within
    normed = norm_rows(tokens.astype(jnp.float32), input_gain).astype(jnp.bfloat16)
    query_latent = norm_rows(
        jnp.dot(normed, query_down, preferred_element_type=jnp.float32), query_gain
    ).astype(jnp.bfloat16)
    query_full = jnp.dot(query_latent, query_up, preferred_element_type=jnp.float32).astype(
        jnp.bfloat16
    )
    query_full = lax.optimization_barrier(query_full).reshape(tok_dev, HEADS, NOPE + ROPE)
    absorbed = jnp.einsum(
        "thd,khd->thk",
        query_full[..., :NOPE],
        key_up.reshape(KVR, HEADS, NOPE),
        preferred_element_type=jnp.float32,
    )
    turned = rotate(query_full[..., NOPE:].astype(jnp.float32), positions)
    queries = jnp.concatenate([absorbed, turned], axis=-1).astype(jnp.bfloat16)
    latent_raw = jnp.dot(normed, latent_down, preferred_element_type=jnp.float32)
    new_latents = jnp.concatenate(
        [norm_rows(latent_raw[:, :KVR], latent_gain), rotate(latent_raw[:, KVR:], positions)],
        axis=-1,
    ).astype(jnp.bfloat16)
    latent_width = new_latents.shape[1]
    span_blocks = lax.axis_size("tq")
    span_rows = lax.all_to_all(
        jnp.broadcast_to(new_latents, (span_blocks,) + new_latents.shape), "tq", 0, 0, tiled=True
    ).reshape(-1, latent_width)
    span_lower = jnp.zeros((tok_dev,), jnp.int32)
    span_limit = within + 1
    cache_rows = lax.all_to_all(
        jnp.tile(cache_latents, (span_blocks, 1, 1)), ("tq", "tr"), 0, 0, tiled=True
    ).reshape(-1, latent_width)
    group_prompts = prompt_of[group_index * group_requests + jnp.arange(group_requests)]
    prompt_send = jnp.take(prompt_latents, group_prompts, axis=0)
    prompt_rows = lax.all_to_all(
        jnp.tile(prompt_send, (span_blocks, 1, 1)), ("tq", "tr"), 0, 0, tiled=True
    ).reshape(-1, latent_width)
    query_rows = queries.reshape(tok_dev * HEADS, latent_width)
    score_scale = 1.0 / (NOPE + ROPE) ** 0.5
    lims = jnp.stack([prompt_live, cache_live]).astype(jnp.int32)
    lim_rows = jnp.repeat(span_limit, HEADS)[:, None]
    latent_out = flash_attend(
        lims, lim_rows, query_rows, prompt_rows, cache_rows, span_rows, score_scale, KVR
    ).reshape(tok_dev, HEADS, KVR)
    heads_out = (
        jnp.einsum(
            "thk,khv->thv",
            latent_out,
            value_up.reshape(KVR, HEADS, VDIM),
            preferred_element_type=jnp.float32,
        )
        .astype(jnp.bfloat16)
        .reshape(tok_dev, HEADS * VDIM)
    )
    attended = jnp.dot(heads_out, output_weight, preferred_element_type=jnp.float32)
    weights_full = lax.all_gather(
        jnp.stack([gate_weight, up_weight, down_weight.T]), ("tq", "tr"), axis=1, tiled=True
    )
    residual, weights_full = lax.optimization_barrier(
        ((tokens.astype(jnp.float32) + attended).astype(jnp.bfloat16), weights_full)
    )
    post_norm = norm_rows(residual.astype(jnp.float32), post_gain).astype(jnp.bfloat16)
    rows_all = lax.all_gather(post_norm, "grp", axis=0, tiled=True)
    gate_full, up_full, down_full = weights_full
    gate_values = jnp.dot(rows_all, gate_full, preferred_element_type=jnp.float32)
    up_values = jnp.dot(rows_all, up_full, preferred_element_type=jnp.float32)
    hidden = (jax.nn.silu(gate_values) * up_values).astype(jnp.bfloat16)
    partial_out = lax.dot_general(
        hidden, down_full, (((1,), (1,)), ((), ())), preferred_element_type=jnp.float32
    )
    down_values = lax.psum_scatter(
        partial_out.astype(jnp.bfloat16), "grp", scatter_dimension=0, tiled=True
    ).astype(jnp.float32)
    layer_out = (residual.astype(jnp.float32) + down_values).astype(jnp.bfloat16)
    return (layer_out, new_latents)


def solution(mesh):
    split = ("grp", "tq", "tr")
    tokens_spec = P(split, None)
    in_specs = (
        tokens_spec,
        P(),
        P(),
        P(),
        P(),
        P(),
        P(),
        P(),
        P(),
        P(),
        P(),
        P(("tq", "tr"), "grp"),
        P(("tq", "tr"), "grp"),
        P("grp", ("tq", "tr")),
        P("grp", ("tq", "tr"), None),
        P(None, ("tq", "tr"), None),
        P(),
        P(),
        P(),
    )
    out_specs = (tokens_spec, tokens_spec)

    def run(*args):
        n_grp, n_tok = mesh.shape["grp"], mesh.shape["tok"]
        tok_dev = args[0].shape[0] // (n_grp * n_tok)
        group_requests = tok_dev * n_tok // SPAN
        sub = Mesh(
            mesh.devices.reshape(n_grp, n_tok // group_requests, group_requests), split
        )
        return jax.shard_map(
            body, mesh=sub, in_specs=in_specs, out_specs=out_specs, check_vma=False
        )(*args)

    return run
```

```python
import jax
import jax.numpy as jnp
from jax import lax
from jax.sharding import Mesh, PartitionSpec as P
import functools
from jax.experimental import pallas as pl
from jax.experimental.pallas import tpu as pltpu

KVR = 256
HEADS = 20
NOPE = 64
ROPE = 32
VDIM = 64
SPAN = 1024


EPSILON = 1e-06


def passed_along(block, axis, distance):
    devices = range(lax.axis_size(axis))
    route = [(i - distance, i) for i in devices if i - distance in devices]
    return lax.ppermute(block, axis, route)


def norm_rows(values, gain_vector):
    mean_square = jnp.mean(values * values, axis=-1, keepdims=True)
    return values * lax.rsqrt(mean_square + EPSILON) * gain_vector.astype(jnp.float32)


def rotate(values, positions):
    half_width = values.shape[-1] // 2
    frequency = 10000.0 ** (-jnp.arange(half_width, dtype=jnp.float32) / half_width)
    angles = positions.astype(jnp.float32)[:, None] * frequency[None, :]
    if values.ndim == 3:
        angles = angles[:, None, :]
    cosine = jnp.cos(angles)
    sine_part = jnp.sin(angles)
    leading = values[..., :half_width]
    trailing = values[..., half_width:]
    return jnp.concatenate(
        [leading * cosine - trailing * sine_part, trailing * cosine + leading * sine_part], axis=-1
    )


KEY_BLOCK = 1024
ROW_BLOCK = 640


def flash_kernel(lims_ref, lim_row_ref, q_ref, kp_ref, kc_ref, ks_ref, o_ref, m_sc, l_sc, acc_sc, *, cache_blocks, score_scale, value_width):
    j = pl.program_id(1)
    last = cache_blocks + 1

    @pl.when(j == 0)
    def _init():
        m_sc[...] = jnp.full(m_sc.shape, -1e30, jnp.float32)
        l_sc[...] = jnp.zeros(l_sc.shape, jnp.float32)
        acc_sc[...] = jnp.zeros(acc_sc.shape, jnp.float32)

    def step(k_ref, base, limit):
        keys = k_ref[...]
        scores = lax.dot_general(q_ref[...], keys, (((1,), (1,)), ((), ())), preferred_element_type=jnp.float32) * score_scale
        place = lax.broadcasted_iota(jnp.int32, scores.shape, 1) + base
        live = place < limit
        m_old = m_sc[...]
        m_new = jnp.maximum(m_old, jnp.max(jnp.where(live, scores, -1e30), axis=1, keepdims=True))
        weights = jnp.where(live, jnp.exp(scores - m_new), 0.0)
        factor = jnp.exp(m_old - m_new)
        l_sc[...] = l_sc[...] * factor + jnp.sum(weights, axis=1, keepdims=True)
        acc_sc[...] = acc_sc[...] * factor + jnp.dot(weights.astype(jnp.bfloat16), keys[:, :value_width], preferred_element_type=jnp.float32)
        m_sc[...] = m_new

    rows = q_ref.shape[0]

    @pl.when(j == 0)
    def _prompt():
        step(kp_ref, 0, jnp.full((rows, 1), lims_ref[0], jnp.int32))

    @pl.when(jnp.logical_and(j >= 1, j < last))
    def _cache():
        step(kc_ref, (j - 1) * KEY_BLOCK, jnp.full((rows, 1), lims_ref[1], jnp.int32))

    @pl.when(j == last)
    def _span():
        step(ks_ref, 0, lim_row_ref[...])
        o_ref[...] = (acc_sc[...] / l_sc[...]).astype(o_ref.dtype)


def flash_attend(lims, lim_rows, queries, prompt_rows, cache_rows, span_rows, score_scale, value_width, interpret=False):
    row_count, width = queries.shape
    cache_blocks = cache_rows.shape[0] // KEY_BLOCK
    assert prompt_rows.shape[0] == KEY_BLOCK and span_rows.shape[0] == KEY_BLOCK
    assert cache_blocks * KEY_BLOCK == cache_rows.shape[0] and row_count % ROW_BLOCK == 0
    grid = (row_count // ROW_BLOCK, cache_blocks + 2)
    key_spec = pl.BlockSpec((KEY_BLOCK, width), lambda i, j, lims: (0, 0))
    cache_spec = pl.BlockSpec((KEY_BLOCK, width), lambda i, j, lims: (jnp.minimum(jnp.maximum(j - 1, 0), cache_blocks - 1), 0))
    kernel = functools.partial(flash_kernel, cache_blocks=cache_blocks, score_scale=score_scale, value_width=value_width)
    return pl.pallas_call(
        kernel,
        grid_spec=pltpu.PrefetchScalarGridSpec(
            num_scalar_prefetch=1,
            grid=grid,
            in_specs=[
                pl.BlockSpec((ROW_BLOCK, 1), lambda i, j, lims: (i, 0)),
                pl.BlockSpec((ROW_BLOCK, width), lambda i, j, lims: (i, 0)),
                key_spec,
                cache_spec,
                key_spec,
            ],
            out_specs=pl.BlockSpec((ROW_BLOCK, value_width), lambda i, j, lims: (i, 0)),
            scratch_shapes=[
                pltpu.VMEM((ROW_BLOCK, 1), jnp.float32),
                pltpu.VMEM((ROW_BLOCK, 1), jnp.float32),
                pltpu.VMEM((ROW_BLOCK, value_width), jnp.float32),
            ],
        ),
        out_shape=jax.ShapeDtypeStruct((row_count, value_width), jnp.bfloat16),
        compiler_params=pltpu.CompilerParams(dimension_semantics=("arbitrary", "arbitrary")),
        interpret=interpret,
    )(lims, lim_rows, queries, prompt_rows, cache_rows, span_rows)


def attend_segment(
    softmax_state, queries, key_rows, lowers, limits, block_count, key_block, score_scale
):

    def fold_block(step_index, carried):
        running_max, running_sum, running_out = carried
        first_key = step_index * key_block
        key_piece = lax.dynamic_slice_in_dim(key_rows, first_key, key_block, 0)
        scores = (
            jnp.einsum("rw,kw->rk", queries, key_piece, preferred_element_type=jnp.float32)
            * score_scale
        )
        key_place = (first_key + jnp.arange(key_block, dtype=jnp.int32))[None, :]
        live_keys = jnp.logical_and(key_place >= lowers[:, None], key_place < limits[:, None])
        next_max = jnp.maximum(running_max, jnp.max(jnp.where(live_keys, scores, -1e30), axis=1))
        weights = jnp.where(live_keys, jnp.exp(scores - next_max[:, None]), 0.0)
        factor = jnp.exp(running_max - next_max)
        running_sum = running_sum * factor + jnp.sum(weights, axis=1)
        running_out = running_out * factor[:, None] + jnp.dot(
            weights.astype(jnp.bfloat16), key_piece[:, :KVR], preferred_element_type=jnp.float32
        )
        return (next_max, running_sum, running_out)

    return lax.fori_loop(0, block_count, fold_block, softmax_state)


def body(
    tokens,
    input_gain,
    query_down,
    query_gain,
    query_up,
    latent_down,
    latent_gain,
    key_up,
    value_up,
    output_weight,
    post_gain,
    gate_weight,
    up_weight,
    down_weight,
    cache_latents,
    prompt_latents,
    cache_len,
    prompt_len,
    prompt_of,
):
    group_index = lax.axis_index("grp")
    span_index = lax.axis_index("tq")
    local_request = lax.axis_index("tr")
    tok_dev = tokens.shape[0]
    group_requests = lax.axis_size("tr")
    owner = group_index * group_requests + local_request
    offset = span_index * tok_dev
    within = offset + jnp.arange(tok_dev, dtype=jnp.int32)
    own_prompt = prompt_of[owner]
    prompt_live = prompt_len[own_prompt]
    cache_live = cache_len[owner]
    positions = prompt_live + cache_live + within
    normed = norm_rows(tokens.astype(jnp.float32), input_gain).astype(jnp.bfloat16)
    query_latent = norm_rows(
        jnp.dot(normed, query_down, preferred_element_type=jnp.float32), query_gain
    ).astype(jnp.bfloat16)
    query_full = jnp.dot(query_latent, query_up, preferred_element_type=jnp.float32).astype(
        jnp.bfloat16
    )
    query_full = lax.optimization_barrier(query_full).reshape(tok_dev, HEADS, NOPE + ROPE)
    absorbed = jnp.einsum(
        "thd,khd->thk",
        query_full[..., :NOPE],
        key_up.reshape(KVR, HEADS, NOPE),
        preferred_element_type=jnp.float32,
    )
    turned = rotate(query_full[..., NOPE:].astype(jnp.float32), positions)
    queries = jnp.concatenate([absorbed, turned], axis=-1).astype(jnp.bfloat16)
    latent_raw = jnp.dot(normed, latent_down, preferred_element_type=jnp.float32)
    new_latents = jnp.concatenate(
        [norm_rows(latent_raw[:, :KVR], latent_gain), rotate(latent_raw[:, KVR:], positions)],
        axis=-1,
    ).astype(jnp.bfloat16)
    latent_width = new_latents.shape[1]
    span_blocks = lax.axis_size("tq")
    span_rows = lax.all_to_all(
        jnp.broadcast_to(new_latents, (span_blocks,) + new_latents.shape), "tq", 0, 0, tiled=True
    ).reshape(-1, latent_width)
    span_lower = jnp.zeros((tok_dev,), jnp.int32)
    span_limit = within + 1
    cache_rows = lax.all_to_all(
        jnp.tile(cache_latents, (span_blocks, 1, 1)), ("tq", "tr"), 0, 0, tiled=True
    ).reshape(-1, latent_width)
    group_prompts = prompt_of[group_index * group_requests + jnp.arange(group_requests)]
    prompt_send = jnp.take(prompt_latents, group_prompts, axis=0)
    prompt_rows = lax.all_to_all(
        jnp.tile(prompt_send, (span_blocks, 1, 1)), ("tq", "tr"), 0, 0, tiled=True
    ).reshape(-1, latent_width)
    query_rows = queries.reshape(tok_dev * HEADS, latent_width)
    score_scale = 1.0 / (NOPE + ROPE) ** 0.5
    lims = jnp.stack([prompt_live, cache_live]).astype(jnp.int32)
    lim_rows = jnp.repeat(span_limit, HEADS)[:, None]
    latent_out = flash_attend(
        lims, lim_rows, query_rows, prompt_rows, cache_rows, span_rows, score_scale, KVR
    ).reshape(tok_dev, HEADS, KVR)
    heads_out = (
        jnp.einsum(
            "thk,khv->thv",
            latent_out,
            value_up.reshape(KVR, HEADS, VDIM),
            preferred_element_type=jnp.float32,
        )
        .astype(jnp.bfloat16)
        .reshape(tok_dev, HEADS * VDIM)
    )
    attended = jnp.dot(heads_out, output_weight, preferred_element_type=jnp.float32)
    weights_full = lax.all_gather(
        jnp.stack([gate_weight, up_weight, down_weight.T]), ("tq", "tr"), axis=1, tiled=True
    )
    residual, weights_full = lax.optimization_barrier(
        ((tokens.astype(jnp.float32) + attended).astype(jnp.bfloat16), weights_full)
    )
    post_norm = norm_rows(residual.astype(jnp.float32), post_gain).astype(jnp.bfloat16)
    half_width = post_norm.shape[1] // 2
    group_count = lax.axis_size("grp")
    rows_all = jnp.concatenate(
        [
            lax.all_gather(post_norm[:, :half_width], "grp", axis=0, tiled=True),
            lax.all_to_all(
                jnp.broadcast_to(
                    post_norm[:, half_width:], (group_count, tok_dev, half_width)
                ),
                "grp",
                0,
                0,
                tiled=True,
            ).reshape(group_count * tok_dev, half_width),
        ],
        axis=1,
    )
    gate_full, up_full, down_full = weights_full
    gate_values = jnp.dot(rows_all, gate_full, preferred_element_type=jnp.float32)
    up_values = jnp.dot(rows_all, up_full, preferred_element_type=jnp.float32)
    hidden = (jax.nn.silu(gate_values) * up_values).astype(jnp.bfloat16)
    partial_out = lax.dot_general(
        hidden, down_full, (((1,), (1,)), ((), ())), preferred_element_type=jnp.float32
    )
    partial_out = partial_out.astype(jnp.bfloat16)
    down_values = jnp.concatenate(
        [
            lax.psum_scatter(
                partial_out[:, :half_width], "grp", scatter_dimension=0, tiled=True
            ).astype(jnp.float32),
            lax.all_to_all(
                partial_out[:, half_width:].reshape(group_count, tok_dev, half_width),
                "grp",
                0,
                0,
                tiled=True,
            )
            .astype(jnp.float32)
            .sum(axis=0),
        ],
        axis=1,
    )
    layer_out = (residual.astype(jnp.float32) + down_values).astype(jnp.bfloat16)
    return (layer_out, new_latents)


def solution(mesh):
    split = ("grp", "tq", "tr")
    tokens_spec = P(split, None)
    in_specs = (
        tokens_spec,
        P(),
        P(),
        P(),
        P(),
        P(),
        P(),
        P(),
        P(),
        P(),
        P(),
        P(("tq", "tr"), "grp"),
        P(("tq", "tr"), "grp"),
        P("grp", ("tq", "tr")),
        P("grp", ("tq", "tr"), None),
        P(None, ("tq", "tr"), None),
        P(),
        P(),
        P(),
    )
    out_specs = (tokens_spec, tokens_spec)

    def run(*args):
        n_grp, n_tok = mesh.shape["grp"], mesh.shape["tok"]
        tok_dev = args[0].shape[0] // (n_grp * n_tok)
        group_requests = tok_dev * n_tok // SPAN
        sub = Mesh(
            mesh.devices.reshape(n_grp, n_tok // group_requests, group_requests), split
        )
        return jax.shard_map(
            body, mesh=sub, in_specs=in_specs, out_specs=out_specs, check_vma=False
        )(*args)

    return run
```

```python
import jax
import jax.numpy as jnp
from jax import lax
from jax.sharding import Mesh, PartitionSpec as P
import functools
from jax.experimental import pallas as pl
from jax.experimental.pallas import tpu as pltpu

KVR = 256
HEADS = 20
NOPE = 64
ROPE = 32
VDIM = 64
SPAN = 1024


EPSILON = 1e-06


def passed_along(block, axis, distance):
    devices = range(lax.axis_size(axis))
    route = [(i - distance, i) for i in devices if i - distance in devices]
    return lax.ppermute(block, axis, route)


def norm_rows(values, gain_vector):
    mean_square = jnp.mean(values * values, axis=-1, keepdims=True)
    return values * lax.rsqrt(mean_square + EPSILON) * gain_vector.astype(jnp.float32)


def rotate(values, positions):
    half_width = values.shape[-1] // 2
    frequency = 10000.0 ** (-jnp.arange(half_width, dtype=jnp.float32) / half_width)
    angles = positions.astype(jnp.float32)[:, None] * frequency[None, :]
    if values.ndim == 3:
        angles = angles[:, None, :]
    cosine = jnp.cos(angles)
    sine_part = jnp.sin(angles)
    leading = values[..., :half_width]
    trailing = values[..., half_width:]
    return jnp.concatenate(
        [leading * cosine - trailing * sine_part, trailing * cosine + leading * sine_part], axis=-1
    )


KEY_BLOCK = 1024
ROW_BLOCK = 640


def flash_kernel(lims_ref, lim_row_ref, q_ref, *refs, plan, first, final, score_scale, value_width):
    key_refs = refs[: len(plan)]
    rest = refs[len(plan) :]
    if not first:
        m_in, l_in, acc_in = rest[:3]
        rest = rest[3:]
    if final:
        o_ref = rest[0]
        rest = rest[1:]
    else:
        m_out, l_out, acc_out = rest[:3]
        rest = rest[3:]
    m_sc, l_sc, acc_sc = rest
    j = pl.program_id(1)
    total = sum(count for _, count in plan)
    rows = q_ref.shape[0]

    @pl.when(j == 0)
    def _init():
        if first:
            m_sc[...] = jnp.full(m_sc.shape, -1e30, jnp.float32)
            l_sc[...] = jnp.zeros(l_sc.shape, jnp.float32)
            acc_sc[...] = jnp.zeros(acc_sc.shape, jnp.float32)
        else:
            m_sc[...] = m_in[...]
            l_sc[...] = l_in[...]
            acc_sc[...] = acc_in[...]

    def step(k_ref, base, limit):
        keys = k_ref[...]
        scores = lax.dot_general(q_ref[...], keys, (((1,), (1,)), ((), ())), preferred_element_type=jnp.float32) * score_scale
        place = lax.broadcasted_iota(jnp.int32, scores.shape, 1) + base
        live = place < limit
        m_old = m_sc[...]
        m_new = jnp.maximum(m_old, jnp.max(jnp.where(live, scores, -1e30), axis=1, keepdims=True))
        weights = jnp.where(live, jnp.exp(scores - m_new), 0.0)
        factor = jnp.exp(m_old - m_new)
        l_sc[...] = l_sc[...] * factor + jnp.sum(weights, axis=1, keepdims=True)
        acc_sc[...] = acc_sc[...] * factor + jnp.dot(weights.astype(jnp.bfloat16), keys[:, :value_width], preferred_element_type=jnp.float32)
        m_sc[...] = m_new

    begin = 0
    for (kind, count), k_ref in zip(plan, key_refs):
        def run(k_ref=k_ref, kind=kind, begin=begin):
            if kind == "span":
                limit = lim_row_ref[...]
            else:
                limit = jnp.full((rows, 1), lims_ref[0 if kind == "prompt" else 1], jnp.int32)
            step(k_ref, (j - begin) * KEY_BLOCK, limit)
        pl.when(jnp.logical_and(j >= begin, j < begin + count))(run)
        begin += count

    @pl.when(j == total - 1)
    def _finish():
        if final:
            o_ref[...] = (acc_sc[...] / l_sc[...]).astype(o_ref.dtype)
        else:
            m_out[...] = m_sc[...]
            l_out[...] = l_sc[...]
            acc_out[...] = acc_sc[...]


def flash_part(lims, lim_rows, queries, segments, state, final, score_scale, value_width, interpret=False):
    row_count, width = queries.shape
    plan = tuple((kind, rows.shape[0] // KEY_BLOCK) for kind, rows in segments)
    total = sum(count for _, count in plan)
    grid = (row_count // ROW_BLOCK, total)
    key_specs = []
    begin = 0
    for _, count in plan:
        key_specs.append(pl.BlockSpec((KEY_BLOCK, width), lambda i, j, lims, b=begin, c=count: (jnp.minimum(jnp.maximum(j - b, 0), c - 1), 0)))
        begin += count
    row_spec = lambda cols: pl.BlockSpec((ROW_BLOCK, cols), lambda i, j, lims: (i, 0))
    in_specs = [row_spec(1), row_spec(width)] + key_specs
    operands = [lims, lim_rows, queries] + [rows for _, rows in segments]
    if state is not None:
        in_specs += [row_spec(1), row_spec(1), row_spec(value_width)]
        operands += list(state)
    if final:
        out_specs = row_spec(value_width)
        out_shape = jax.ShapeDtypeStruct((row_count, value_width), jnp.bfloat16)
    else:
        out_specs = [row_spec(1), row_spec(1), row_spec(value_width)]
        out_shape = [
            jax.ShapeDtypeStruct((row_count, 1), jnp.float32),
            jax.ShapeDtypeStruct((row_count, 1), jnp.float32),
            jax.ShapeDtypeStruct((row_count, value_width), jnp.float32),
        ]
    key_count = total * KEY_BLOCK
    kernel = functools.partial(flash_kernel, plan=plan, first=state is None, final=final, score_scale=score_scale, value_width=value_width)
    return pl.pallas_call(
        kernel,
        grid_spec=pltpu.PrefetchScalarGridSpec(
            num_scalar_prefetch=1,
            grid=grid,
            in_specs=in_specs,
            out_specs=out_specs,
            scratch_shapes=[
                pltpu.VMEM((ROW_BLOCK, 1), jnp.float32),
                pltpu.VMEM((ROW_BLOCK, 1), jnp.float32),
                pltpu.VMEM((ROW_BLOCK, value_width), jnp.float32),
            ],
        ),
        out_shape=out_shape,
        compiler_params=pltpu.CompilerParams(dimension_semantics=("arbitrary", "arbitrary")),
        interpret=interpret,
        cost_estimate=pl.CostEstimate(
            flops=2 * row_count * key_count * (width + value_width),
            transcendentals=row_count * key_count,
            bytes_accessed=2 * (row_count * (width + value_width) + key_count * width),
        ),
    )(*operands)


def attend_segment(
    softmax_state, queries, key_rows, lowers, limits, block_count, key_block, score_scale
):

    def fold_block(step_index, carried):
        running_max, running_sum, running_out = carried
        first_key = step_index * key_block
        key_piece = lax.dynamic_slice_in_dim(key_rows, first_key, key_block, 0)
        scores = (
            jnp.einsum("rw,kw->rk", queries, key_piece, preferred_element_type=jnp.float32)
            * score_scale
        )
        key_place = (first_key + jnp.arange(key_block, dtype=jnp.int32))[None, :]
        live_keys = jnp.logical_and(key_place >= lowers[:, None], key_place < limits[:, None])
        next_max = jnp.maximum(running_max, jnp.max(jnp.where(live_keys, scores, -1e30), axis=1))
        weights = jnp.where(live_keys, jnp.exp(scores - next_max[:, None]), 0.0)
        factor = jnp.exp(running_max - next_max)
        running_sum = running_sum * factor + jnp.sum(weights, axis=1)
        running_out = running_out * factor[:, None] + jnp.dot(
            weights.astype(jnp.bfloat16), key_piece[:, :KVR], preferred_element_type=jnp.float32
        )
        return (next_max, running_sum, running_out)

    return lax.fori_loop(0, block_count, fold_block, softmax_state)


def body(
    tokens,
    input_gain,
    query_down,
    query_gain,
    query_up,
    latent_down,
    latent_gain,
    key_up,
    value_up,
    output_weight,
    post_gain,
    gate_weight,
    up_weight,
    down_weight,
    cache_latents,
    prompt_latents,
    cache_len,
    prompt_len,
    prompt_of,
):
    group_index = lax.axis_index("grp")
    span_index = lax.axis_index("tq")
    local_request = lax.axis_index("tr")
    tok_dev = tokens.shape[0]
    group_requests = lax.axis_size("tr")
    owner = group_index * group_requests + local_request
    offset = span_index * tok_dev
    within = offset + jnp.arange(tok_dev, dtype=jnp.int32)
    own_prompt = prompt_of[owner]
    prompt_live = prompt_len[own_prompt]
    cache_live = cache_len[owner]
    positions = prompt_live + cache_live + within
    normed = norm_rows(tokens.astype(jnp.float32), input_gain).astype(jnp.bfloat16)
    query_latent = norm_rows(
        jnp.dot(normed, query_down, preferred_element_type=jnp.float32), query_gain
    ).astype(jnp.bfloat16)
    query_full = jnp.dot(query_latent, query_up, preferred_element_type=jnp.float32).astype(
        jnp.bfloat16
    )
    query_full = lax.optimization_barrier(query_full).reshape(tok_dev, HEADS, NOPE + ROPE)
    absorbed = jnp.einsum(
        "thd,khd->thk",
        query_full[..., :NOPE],
        key_up.reshape(KVR, HEADS, NOPE),
        preferred_element_type=jnp.float32,
    )
    turned = rotate(query_full[..., NOPE:].astype(jnp.float32), positions)
    queries = jnp.concatenate([absorbed, turned], axis=-1).astype(jnp.bfloat16)
    latent_raw = jnp.dot(normed, latent_down, preferred_element_type=jnp.float32)
    new_latents = jnp.concatenate(
        [norm_rows(latent_raw[:, :KVR], latent_gain), rotate(latent_raw[:, KVR:], positions)],
        axis=-1,
    ).astype(jnp.bfloat16)
    latent_width = new_latents.shape[1]
    span_blocks = lax.axis_size("tq")
    span_rows = lax.all_to_all(
        jnp.broadcast_to(new_latents, (span_blocks,) + new_latents.shape), "tq", 0, 0, tiled=True
    ).reshape(-1, latent_width)
    span_lower = jnp.zeros((tok_dev,), jnp.int32)
    span_limit = within + 1
    group_prompts = prompt_of[group_index * group_requests + jnp.arange(group_requests)]
    prompt_send = jnp.take(prompt_latents, group_prompts, axis=0)
    prompt_rows = lax.all_to_all(
        jnp.tile(prompt_send, (span_blocks, 1, 1)), ("tq", "tr"), 0, 0, tiled=True
    ).reshape(-1, latent_width)
    cache_send, _ = lax.optimization_barrier(
        (jnp.tile(cache_latents, (span_blocks, 1, 1)), prompt_rows)
    )
    cache_rows = lax.all_to_all(cache_send, ("tq", "tr"), 0, 0, tiled=True).reshape(
        -1, latent_width
    )
    query_rows = queries.reshape(tok_dev * HEADS, latent_width)
    score_scale = 1.0 / (NOPE + ROPE) ** 0.5
    lims = jnp.stack([prompt_live, cache_live]).astype(jnp.int32)
    lim_rows = jnp.repeat(span_limit, HEADS)[:, None]
    early_state = flash_part(
        lims,
        lim_rows,
        query_rows,
        (("span", span_rows), ("prompt", prompt_rows)),
        None,
        False,
        score_scale,
        KVR,
    )
    latent_out = flash_part(
        lims, lim_rows, query_rows, (("cache", cache_rows),), early_state, True, score_scale, KVR
    ).reshape(tok_dev, HEADS, KVR)
    heads_out = (
        jnp.einsum(
            "thk,khv->thv",
            latent_out,
            value_up.reshape(KVR, HEADS, VDIM),
            preferred_element_type=jnp.float32,
        )
        .astype(jnp.bfloat16)
        .reshape(tok_dev, HEADS * VDIM)
    )
    attended = jnp.dot(heads_out, output_weight, preferred_element_type=jnp.float32)
    weights_full = lax.all_gather(
        jnp.stack([gate_weight, up_weight, down_weight.T]), ("tq", "tr"), axis=1, tiled=True
    )
    residual, weights_full = lax.optimization_barrier(
        ((tokens.astype(jnp.float32) + attended).astype(jnp.bfloat16), weights_full)
    )
    post_norm = norm_rows(residual.astype(jnp.float32), post_gain).astype(jnp.bfloat16)
    half_width = post_norm.shape[1] // 2
    group_count = lax.axis_size("grp")
    rows_all = jnp.concatenate(
        [
            lax.all_gather(post_norm[:, :half_width], "grp", axis=0, tiled=True),
            lax.all_to_all(
                jnp.broadcast_to(
                    post_norm[:, half_width:], (group_count, tok_dev, half_width)
                ),
                "grp",
                0,
                0,
                tiled=True,
            ).reshape(group_count * tok_dev, half_width),
        ],
        axis=1,
    )
    gate_full, up_full, down_full = weights_full
    gate_values = jnp.dot(rows_all, gate_full, preferred_element_type=jnp.float32)
    up_values = jnp.dot(rows_all, up_full, preferred_element_type=jnp.float32)
    hidden = (jax.nn.silu(gate_values) * up_values).astype(jnp.bfloat16)
    partial_out = lax.dot_general(
        hidden, down_full, (((1,), (1,)), ((), ())), preferred_element_type=jnp.float32
    )
    partial_out = partial_out.astype(jnp.bfloat16)
    down_values = jnp.concatenate(
        [
            lax.psum_scatter(
                partial_out[:, :half_width], "grp", scatter_dimension=0, tiled=True
            ).astype(jnp.float32),
            lax.all_to_all(
                partial_out[:, half_width:].reshape(group_count, tok_dev, half_width),
                "grp",
                0,
                0,
                tiled=True,
            )
            .astype(jnp.float32)
            .sum(axis=0),
        ],
        axis=1,
    )
    layer_out = (residual.astype(jnp.float32) + down_values).astype(jnp.bfloat16)
    return (layer_out, new_latents)


def solution(mesh):
    split = ("grp", "tq", "tr")
    tokens_spec = P(split, None)
    in_specs = (
        tokens_spec,
        P(),
        P(),
        P(),
        P(),
        P(),
        P(),
        P(),
        P(),
        P(),
        P(),
        P(("tq", "tr"), "grp"),
        P(("tq", "tr"), "grp"),
        P("grp", ("tq", "tr")),
        P("grp", ("tq", "tr"), None),
        P(None, ("tq", "tr"), None),
        P(),
        P(),
        P(),
    )
    out_specs = (tokens_spec, tokens_spec)

    def run(*args):
        n_grp, n_tok = mesh.shape["grp"], mesh.shape["tok"]
        tok_dev = args[0].shape[0] // (n_grp * n_tok)
        group_requests = tok_dev * n_tok // SPAN
        sub = Mesh(
            mesh.devices.reshape(n_grp, n_tok // group_requests, group_requests), split
        )
        return jax.shard_map(
            body, mesh=sub, in_specs=in_specs, out_specs=out_specs, check_vma=False
        )(*args)

    return run
```

```python
import jax
import jax.numpy as jnp
from jax import lax
from jax.sharding import Mesh, PartitionSpec as P
import functools
from jax.experimental import pallas as pl
from jax.experimental.pallas import tpu as pltpu

KVR = 256
HEADS = 20
NOPE = 64
ROPE = 32
VDIM = 64
SPAN = 1024


EPSILON = 1e-06


def passed_along(block, axis, distance):
    devices = range(lax.axis_size(axis))
    route = [(i - distance, i) for i in devices if i - distance in devices]
    return lax.ppermute(block, axis, route)


def norm_rows(values, gain_vector):
    mean_square = jnp.mean(values * values, axis=-1, keepdims=True)
    return values * lax.rsqrt(mean_square + EPSILON) * gain_vector.astype(jnp.float32)


def rotate(values, positions):
    half_width = values.shape[-1] // 2
    frequency = 10000.0 ** (-jnp.arange(half_width, dtype=jnp.float32) / half_width)
    angles = positions.astype(jnp.float32)[:, None] * frequency[None, :]
    if values.ndim == 3:
        angles = angles[:, None, :]
    cosine = jnp.cos(angles)
    sine_part = jnp.sin(angles)
    leading = values[..., :half_width]
    trailing = values[..., half_width:]
    return jnp.concatenate(
        [leading * cosine - trailing * sine_part, trailing * cosine + leading * sine_part], axis=-1
    )


KEY_BLOCK = 1024
ROW_BLOCK = 640


def flash_kernel(lims_ref, lim_row_ref, q_ref, *refs, plan, first, final, score_scale, value_width):
    key_refs = refs[: len(plan)]
    rest = refs[len(plan) :]
    if not first:
        m_in, l_in, acc_in = rest[:3]
        rest = rest[3:]
    if final:
        o_ref = rest[0]
        rest = rest[1:]
    else:
        m_out, l_out, acc_out = rest[:3]
        rest = rest[3:]
    m_sc, l_sc, acc_sc = rest
    j = pl.program_id(1)
    total = sum(count for _, count in plan)
    rows = q_ref.shape[0]

    @pl.when(j == 0)
    def _init():
        if first:
            m_sc[...] = jnp.full(m_sc.shape, -1e30, jnp.float32)
            l_sc[...] = jnp.zeros(l_sc.shape, jnp.float32)
            acc_sc[...] = jnp.zeros(acc_sc.shape, jnp.float32)
        else:
            m_sc[...] = m_in[...]
            l_sc[...] = l_in[...]
            acc_sc[...] = acc_in[...]

    def step(k_ref, base, limit, masked=True):
        keys = k_ref[...]
        scores = lax.dot_general(q_ref[...], keys, (((1,), (1,)), ((), ())), preferred_element_type=jnp.float32) * score_scale
        m_old = m_sc[...]
        if masked:
            place = lax.broadcasted_iota(jnp.int32, scores.shape, 1) + base
            live = place < limit
            m_new = jnp.maximum(m_old, jnp.max(jnp.where(live, scores, -1e30), axis=1, keepdims=True))
            weights = jnp.where(live, jnp.exp(scores - m_new), 0.0)
        else:
            m_new = jnp.maximum(m_old, jnp.max(scores, axis=1, keepdims=True))
            weights = jnp.exp(scores - m_new)
        factor = jnp.exp(m_old - m_new)
        l_sc[...] = l_sc[...] * factor + jnp.sum(weights, axis=1, keepdims=True)
        acc_sc[...] = acc_sc[...] * factor + jnp.dot(weights.astype(jnp.bfloat16), keys[:, :value_width], preferred_element_type=jnp.float32)
        m_sc[...] = m_new

    begin = 0
    for (kind, count), k_ref in zip(plan, key_refs):
        inside = jnp.logical_and(j >= begin, j < begin + count)
        base = (j - begin) * KEY_BLOCK
        if kind == "span":
            pl.when(inside)(functools.partial(step, k_ref, base, lim_row_ref[...]))
        else:
            live_rows = lims_ref[0 if kind == "prompt" else 1]
            whole = base + KEY_BLOCK <= live_rows
            part = jnp.logical_and(jnp.logical_not(whole), base < live_rows)
            pl.when(jnp.logical_and(inside, whole))(
                functools.partial(step, k_ref, base, live_rows, False)
            )
            pl.when(jnp.logical_and(inside, part))(
                functools.partial(step, k_ref, base, jnp.full((rows, 1), live_rows, jnp.int32))
            )
        begin += count

    @pl.when(j == total - 1)
    def _finish():
        if final:
            o_ref[...] = (acc_sc[...] / l_sc[...]).astype(o_ref.dtype)
        else:
            m_out[...] = m_sc[...]
            l_out[...] = l_sc[...]
            acc_out[...] = acc_sc[...]


def flash_part(lims, lim_rows, queries, segments, state, final, score_scale, value_width, interpret=False):
    row_count, width = queries.shape
    plan = tuple((kind, rows.shape[0] // KEY_BLOCK) for kind, rows in segments)
    total = sum(count for _, count in plan)
    grid = (row_count // ROW_BLOCK, total)
    key_specs = []
    begin = 0
    for _, count in plan:
        key_specs.append(pl.BlockSpec((KEY_BLOCK, width), lambda i, j, lims, b=begin, c=count: (jnp.minimum(jnp.maximum(j - b, 0), c - 1), 0)))
        begin += count
    row_spec = lambda cols: pl.BlockSpec((ROW_BLOCK, cols), lambda i, j, lims: (i, 0))
    in_specs = [row_spec(1), row_spec(width)] + key_specs
    operands = [lims, lim_rows, queries] + [rows for _, rows in segments]
    if state is not None:
        in_specs += [row_spec(1), row_spec(1), row_spec(value_width)]
        operands += list(state)
    if final:
        out_specs = row_spec(value_width)
        out_shape = jax.ShapeDtypeStruct((row_count, value_width), jnp.bfloat16)
    else:
        out_specs = [row_spec(1), row_spec(1), row_spec(value_width)]
        out_shape = [
            jax.ShapeDtypeStruct((row_count, 1), jnp.float32),
            jax.ShapeDtypeStruct((row_count, 1), jnp.float32),
            jax.ShapeDtypeStruct((row_count, value_width), jnp.float32),
        ]
    key_count = total * KEY_BLOCK
    kernel = functools.partial(flash_kernel, plan=plan, first=state is None, final=final, score_scale=score_scale, value_width=value_width)
    return pl.pallas_call(
        kernel,
        grid_spec=pltpu.PrefetchScalarGridSpec(
            num_scalar_prefetch=1,
            grid=grid,
            in_specs=in_specs,
            out_specs=out_specs,
            scratch_shapes=[
                pltpu.VMEM((ROW_BLOCK, 1), jnp.float32),
                pltpu.VMEM((ROW_BLOCK, 1), jnp.float32),
                pltpu.VMEM((ROW_BLOCK, value_width), jnp.float32),
            ],
        ),
        out_shape=out_shape,
        compiler_params=pltpu.CompilerParams(dimension_semantics=("arbitrary", "arbitrary")),
        interpret=interpret,
        cost_estimate=pl.CostEstimate(
            flops=2 * row_count * key_count * (width + value_width),
            transcendentals=row_count * key_count,
            bytes_accessed=2 * (row_count * (width + value_width) + key_count * width),
        ),
    )(*operands)


def attend_segment(
    softmax_state, queries, key_rows, lowers, limits, block_count, key_block, score_scale
):

    def fold_block(step_index, carried):
        running_max, running_sum, running_out = carried
        first_key = step_index * key_block
        key_piece = lax.dynamic_slice_in_dim(key_rows, first_key, key_block, 0)
        scores = (
            jnp.einsum("rw,kw->rk", queries, key_piece, preferred_element_type=jnp.float32)
            * score_scale
        )
        key_place = (first_key + jnp.arange(key_block, dtype=jnp.int32))[None, :]
        live_keys = jnp.logical_and(key_place >= lowers[:, None], key_place < limits[:, None])
        next_max = jnp.maximum(running_max, jnp.max(jnp.where(live_keys, scores, -1e30), axis=1))
        weights = jnp.where(live_keys, jnp.exp(scores - next_max[:, None]), 0.0)
        factor = jnp.exp(running_max - next_max)
        running_sum = running_sum * factor + jnp.sum(weights, axis=1)
        running_out = running_out * factor[:, None] + jnp.dot(
            weights.astype(jnp.bfloat16), key_piece[:, :KVR], preferred_element_type=jnp.float32
        )
        return (next_max, running_sum, running_out)

    return lax.fori_loop(0, block_count, fold_block, softmax_state)


def body(
    tokens,
    input_gain,
    query_down,
    query_gain,
    query_up,
    latent_down,
    latent_gain,
    key_up,
    value_up,
    output_weight,
    post_gain,
    gate_weight,
    up_weight,
    down_weight,
    cache_latents,
    prompt_latents,
    cache_len,
    prompt_len,
    prompt_of,
):
    group_index = lax.axis_index("grp")
    span_index = lax.axis_index("tq")
    local_request = lax.axis_index("tr")
    tok_dev = tokens.shape[0]
    group_requests = lax.axis_size("tr")
    owner = group_index * group_requests + local_request
    offset = span_index * tok_dev
    within = offset + jnp.arange(tok_dev, dtype=jnp.int32)
    own_prompt = prompt_of[owner]
    prompt_live = prompt_len[own_prompt]
    cache_live = cache_len[owner]
    positions = prompt_live + cache_live + within
    normed = norm_rows(tokens.astype(jnp.float32), input_gain).astype(jnp.bfloat16)
    query_latent = norm_rows(
        jnp.dot(normed, query_down, preferred_element_type=jnp.float32), query_gain
    ).astype(jnp.bfloat16)
    query_full = jnp.dot(query_latent, query_up, preferred_element_type=jnp.float32).astype(
        jnp.bfloat16
    )
    query_full = lax.optimization_barrier(query_full).reshape(tok_dev, HEADS, NOPE + ROPE)
    absorbed = jnp.einsum(
        "thd,khd->thk",
        query_full[..., :NOPE],
        key_up.reshape(KVR, HEADS, NOPE),
        preferred_element_type=jnp.float32,
    )
    turned = rotate(query_full[..., NOPE:].astype(jnp.float32), positions)
    queries = jnp.concatenate([absorbed, turned], axis=-1).astype(jnp.bfloat16)
    latent_raw = jnp.dot(normed, latent_down, preferred_element_type=jnp.float32)
    new_latents = jnp.concatenate(
        [norm_rows(latent_raw[:, :KVR], latent_gain), rotate(latent_raw[:, KVR:], positions)],
        axis=-1,
    ).astype(jnp.bfloat16)
    latent_width = new_latents.shape[1]
    span_blocks = lax.axis_size("tq")
    span_rows = lax.all_to_all(
        jnp.broadcast_to(new_latents, (span_blocks,) + new_latents.shape), "tq", 0, 0, tiled=True
    ).reshape(-1, latent_width)
    span_lower = jnp.zeros((tok_dev,), jnp.int32)
    span_limit = within + 1
    group_prompts = prompt_of[group_index * group_requests + jnp.arange(group_requests)]
    prompt_send = jnp.take(prompt_latents, group_prompts, axis=0)
    prompt_rows = lax.all_to_all(
        jnp.tile(prompt_send, (span_blocks, 1, 1)), ("tq", "tr"), 0, 0, tiled=True
    ).reshape(-1, latent_width)
    cache_send, _ = lax.optimization_barrier(
        (jnp.tile(cache_latents, (span_blocks, 1, 1)), prompt_rows)
    )
    cache_rows = lax.all_to_all(cache_send, ("tq", "tr"), 0, 0, tiled=True).reshape(
        -1, latent_width
    )
    query_rows = queries.reshape(tok_dev * HEADS, latent_width)
    score_scale = 1.0 / (NOPE + ROPE) ** 0.5
    lims = jnp.stack([prompt_live, cache_live]).astype(jnp.int32)
    lim_rows = jnp.repeat(span_limit, HEADS)[:, None]
    early_state = flash_part(
        lims,
        lim_rows,
        query_rows,
        (("span", span_rows), ("prompt", prompt_rows)),
        None,
        False,
        score_scale,
        KVR,
    )
    latent_out = flash_part(
        lims, lim_rows, query_rows, (("cache", cache_rows),), early_state, True, score_scale, KVR
    ).reshape(tok_dev, HEADS, KVR)
    heads_out = (
        jnp.einsum(
            "thk,khv->thv",
            latent_out,
            value_up.reshape(KVR, HEADS, VDIM),
            preferred_element_type=jnp.float32,
        )
        .astype(jnp.bfloat16)
        .reshape(tok_dev, HEADS * VDIM)
    )
    attended = jnp.dot(heads_out, output_weight, preferred_element_type=jnp.float32)
    weights_full = lax.all_gather(
        jnp.stack([gate_weight, up_weight, down_weight.T]), ("tq", "tr"), axis=1, tiled=True
    )
    residual, weights_full = lax.optimization_barrier(
        ((tokens.astype(jnp.float32) + attended).astype(jnp.bfloat16), weights_full)
    )
    post_norm = norm_rows(residual.astype(jnp.float32), post_gain).astype(jnp.bfloat16)
    half_width = post_norm.shape[1] // 2
    group_count = lax.axis_size("grp")
    rows_all = jnp.concatenate(
        [
            lax.all_gather(post_norm[:, :half_width], "grp", axis=0, tiled=True),
            lax.all_to_all(
                jnp.broadcast_to(
                    post_norm[:, half_width:], (group_count, tok_dev, half_width)
                ),
                "grp",
                0,
                0,
                tiled=True,
            ).reshape(group_count * tok_dev, half_width),
        ],
        axis=1,
    )
    gate_full, up_full, down_full = weights_full
    gate_values = jnp.dot(rows_all, gate_full, preferred_element_type=jnp.float32)
    up_values = jnp.dot(rows_all, up_full, preferred_element_type=jnp.float32)
    hidden = (jax.nn.silu(gate_values) * up_values).astype(jnp.bfloat16)
    partial_out = lax.dot_general(
        hidden, down_full, (((1,), (1,)), ((), ())), preferred_element_type=jnp.float32
    )
    partial_out = partial_out.astype(jnp.bfloat16)
    down_values = jnp.concatenate(
        [
            lax.psum_scatter(
                partial_out[:, :half_width], "grp", scatter_dimension=0, tiled=True
            ).astype(jnp.float32),
            lax.all_to_all(
                partial_out[:, half_width:].reshape(group_count, tok_dev, half_width),
                "grp",
                0,
                0,
                tiled=True,
            )
            .astype(jnp.float32)
            .sum(axis=0),
        ],
        axis=1,
    )
    layer_out = (residual.astype(jnp.float32) + down_values).astype(jnp.bfloat16)
    return (layer_out, new_latents)


def solution(mesh):
    split = ("grp", "tq", "tr")
    tokens_spec = P(split, None)
    in_specs = (
        tokens_spec,
        P(),
        P(),
        P(),
        P(),
        P(),
        P(),
        P(),
        P(),
        P(),
        P(),
        P(("tq", "tr"), "grp"),
        P(("tq", "tr"), "grp"),
        P("grp", ("tq", "tr")),
        P("grp", ("tq", "tr"), None),
        P(None, ("tq", "tr"), None),
        P(),
        P(),
        P(),
    )
    out_specs = (tokens_spec, tokens_spec)

    def run(*args):
        n_grp, n_tok = mesh.shape["grp"], mesh.shape["tok"]
        tok_dev = args[0].shape[0] // (n_grp * n_tok)
        group_requests = tok_dev * n_tok // SPAN
        sub = Mesh(
            mesh.devices.reshape(n_grp, n_tok // group_requests, group_requests), split
        )
        return jax.shard_map(
            body, mesh=sub, in_specs=in_specs, out_specs=out_specs, check_vma=False
        )(*args)

    return run
```

```python
import jax
import jax.numpy as jnp
from jax import lax
from jax.sharding import Mesh, PartitionSpec as P
import functools
from jax.experimental import pallas as pl
from jax.experimental.pallas import tpu as pltpu

KVR = 256
HEADS = 20
NOPE = 64
ROPE = 32
VDIM = 64
SPAN = 1024


EPSILON = 1e-06


def passed_along(block, axis, distance):
    devices = range(lax.axis_size(axis))
    route = [(i - distance, i) for i in devices if i - distance in devices]
    return lax.ppermute(block, axis, route)


def norm_rows(values, gain_vector):
    mean_square = jnp.mean(values * values, axis=-1, keepdims=True)
    return values * lax.rsqrt(mean_square + EPSILON) * gain_vector.astype(jnp.float32)


def rotate(values, positions):
    half_width = values.shape[-1] // 2
    frequency = 10000.0 ** (-jnp.arange(half_width, dtype=jnp.float32) / half_width)
    angles = positions.astype(jnp.float32)[:, None] * frequency[None, :]
    if values.ndim == 3:
        angles = angles[:, None, :]
    cosine = jnp.cos(angles)
    sine_part = jnp.sin(angles)
    leading = values[..., :half_width]
    trailing = values[..., half_width:]
    return jnp.concatenate(
        [leading * cosine - trailing * sine_part, trailing * cosine + leading * sine_part], axis=-1
    )


KEY_BLOCK = 1024
ROW_BLOCK = 1280


def flash_kernel(lims_ref, lim_row_ref, q_ref, *refs, plan, first, final, score_scale, value_width):
    key_refs = refs[: len(plan)]
    rest = refs[len(plan) :]
    if not first:
        m_in, l_in, acc_in = rest[:3]
        rest = rest[3:]
    if final:
        o_ref = rest[0]
        rest = rest[1:]
    else:
        m_out, l_out, acc_out = rest[:3]
        rest = rest[3:]
    m_sc, l_sc, acc_sc = rest
    j = pl.program_id(1)
    total = sum(count for _, count in plan)
    rows = q_ref.shape[0]

    @pl.when(j == 0)
    def _init():
        if first:
            m_sc[...] = jnp.full(m_sc.shape, -1e30, jnp.float32)
            l_sc[...] = jnp.zeros(l_sc.shape, jnp.float32)
            acc_sc[...] = jnp.zeros(acc_sc.shape, jnp.float32)
        else:
            m_sc[...] = m_in[...]
            l_sc[...] = l_in[...]
            acc_sc[...] = acc_in[...]

    def step(k_ref, base, limit):
        keys = k_ref[...]
        scores = lax.dot_general(q_ref[...], keys, (((1,), (1,)), ((), ())), preferred_element_type=jnp.float32) * score_scale
        place = lax.broadcasted_iota(jnp.int32, scores.shape, 1) + base
        live = place < limit
        m_old = m_sc[...]
        m_new = jnp.maximum(m_old, jnp.max(jnp.where(live, scores, -1e30), axis=1, keepdims=True))
        weights = jnp.where(live, jnp.exp(scores - m_new), 0.0)
        factor = jnp.exp(m_old - m_new)
        l_sc[...] = l_sc[...] * factor + jnp.sum(weights, axis=1, keepdims=True)
        acc_sc[...] = acc_sc[...] * factor + jnp.dot(weights.astype(jnp.bfloat16), keys[:, :value_width], preferred_element_type=jnp.float32)
        m_sc[...] = m_new

    begin = 0
    for (kind, count), k_ref in zip(plan, key_refs):
        def run(k_ref=k_ref, kind=kind, begin=begin):
            if kind == "span":
                limit = lim_row_ref[...]
            else:
                limit = jnp.full((rows, 1), lims_ref[0 if kind == "prompt" else 1], jnp.int32)
            step(k_ref, (j - begin) * KEY_BLOCK, limit)
        pl.when(jnp.logical_and(j >= begin, j < begin + count))(run)
        begin += count

    @pl.when(j == total - 1)
    def _finish():
        if final:
            o_ref[...] = (acc_sc[...] / l_sc[...]).astype(o_ref.dtype)
        else:
            m_out[...] = m_sc[...]
            l_out[...] = l_sc[...]
            acc_out[...] = acc_sc[...]


def flash_part(lims, lim_rows, queries, segments, state, final, score_scale, value_width, interpret=False):
    row_count, width = queries.shape
    plan = tuple((kind, rows.shape[0] // KEY_BLOCK) for kind, rows in segments)
    total = sum(count for _, count in plan)
    grid = (row_count // ROW_BLOCK, total)
    key_specs = []
    begin = 0
    for _, count in plan:
        key_specs.append(pl.BlockSpec((KEY_BLOCK, width), lambda i, j, lims, b=begin, c=count: (jnp.minimum(jnp.maximum(j - b, 0), c - 1), 0)))
        begin += count
    row_spec = lambda cols: pl.BlockSpec((ROW_BLOCK, cols), lambda i, j, lims: (i, 0))
    in_specs = [row_spec(1), row_spec(width)] + key_specs
    operands = [lims, lim_rows, queries] + [rows for _, rows in segments]
    if state is not None:
        in_specs += [row_spec(1), row_spec(1), row_spec(value_width)]
        operands += list(state)
    if final:
        out_specs = row_spec(value_width)
        out_shape = jax.ShapeDtypeStruct((row_count, value_width), jnp.bfloat16)
    else:
        out_specs = [row_spec(1), row_spec(1), row_spec(value_width)]
        out_shape = [
            jax.ShapeDtypeStruct((row_count, 1), jnp.float32),
            jax.ShapeDtypeStruct((row_count, 1), jnp.float32),
            jax.ShapeDtypeStruct((row_count, value_width), jnp.float32),
        ]
    key_count = total * KEY_BLOCK
    kernel = functools.partial(flash_kernel, plan=plan, first=state is None, final=final, score_scale=score_scale, value_width=value_width)
    return pl.pallas_call(
        kernel,
        grid_spec=pltpu.PrefetchScalarGridSpec(
            num_scalar_prefetch=1,
            grid=grid,
            in_specs=in_specs,
            out_specs=out_specs,
            scratch_shapes=[
                pltpu.VMEM((ROW_BLOCK, 1), jnp.float32),
                pltpu.VMEM((ROW_BLOCK, 1), jnp.float32),
                pltpu.VMEM((ROW_BLOCK, value_width), jnp.float32),
            ],
        ),
        out_shape=out_shape,
        compiler_params=pltpu.CompilerParams(dimension_semantics=("arbitrary", "arbitrary")),
        interpret=interpret,
        cost_estimate=pl.CostEstimate(
            flops=2 * row_count * key_count * (width + value_width),
            transcendentals=row_count * key_count,
            bytes_accessed=2 * (row_count * (width + value_width) + key_count * width),
        ),
    )(*operands)


def attend_segment(
    softmax_state, queries, key_rows, lowers, limits, block_count, key_block, score_scale
):

    def fold_block(step_index, carried):
        running_max, running_sum, running_out = carried
        first_key = step_index * key_block
        key_piece = lax.dynamic_slice_in_dim(key_rows, first_key, key_block, 0)
        scores = (
            jnp.einsum("rw,kw->rk", queries, key_piece, preferred_element_type=jnp.float32)
            * score_scale
        )
        key_place = (first_key + jnp.arange(key_block, dtype=jnp.int32))[None, :]
        live_keys = jnp.logical_and(key_place >= lowers[:, None], key_place < limits[:, None])
        next_max = jnp.maximum(running_max, jnp.max(jnp.where(live_keys, scores, -1e30), axis=1))
        weights = jnp.where(live_keys, jnp.exp(scores - next_max[:, None]), 0.0)
        factor = jnp.exp(running_max - next_max)
        running_sum = running_sum * factor + jnp.sum(weights, axis=1)
        running_out = running_out * factor[:, None] + jnp.dot(
            weights.astype(jnp.bfloat16), key_piece[:, :KVR], preferred_element_type=jnp.float32
        )
        return (next_max, running_sum, running_out)

    return lax.fori_loop(0, block_count, fold_block, softmax_state)


def body(
    tokens,
    input_gain,
    query_down,
    query_gain,
    query_up,
    latent_down,
    latent_gain,
    key_up,
    value_up,
    output_weight,
    post_gain,
    gate_weight,
    up_weight,
    down_weight,
    cache_latents,
    prompt_latents,
    cache_len,
    prompt_len,
    prompt_of,
):
    group_index = lax.axis_index("grp")
    span_index = lax.axis_index("tq")
    local_request = lax.axis_index("tr")
    tok_dev = tokens.shape[0]
    group_requests = lax.axis_size("tr")
    owner = group_index * group_requests + local_request
    offset = span_index * tok_dev
    within = offset + jnp.arange(tok_dev, dtype=jnp.int32)
    own_prompt = prompt_of[owner]
    prompt_live = prompt_len[own_prompt]
    cache_live = cache_len[owner]
    positions = prompt_live + cache_live + within
    normed = norm_rows(tokens.astype(jnp.float32), input_gain).astype(jnp.bfloat16)
    query_latent = norm_rows(
        jnp.dot(normed, query_down, preferred_element_type=jnp.float32), query_gain
    ).astype(jnp.bfloat16)
    query_full = jnp.dot(query_latent, query_up, preferred_element_type=jnp.float32).astype(
        jnp.bfloat16
    )
    query_full = lax.optimization_barrier(query_full).reshape(tok_dev, HEADS, NOPE + ROPE)
    absorbed = jnp.einsum(
        "thd,khd->thk",
        query_full[..., :NOPE],
        key_up.reshape(KVR, HEADS, NOPE),
        preferred_element_type=jnp.float32,
    )
    turned = rotate(query_full[..., NOPE:].astype(jnp.float32), positions)
    queries = jnp.concatenate([absorbed, turned], axis=-1).astype(jnp.bfloat16)
    latent_raw = jnp.dot(normed, latent_down, preferred_element_type=jnp.float32)
    new_latents = jnp.concatenate(
        [norm_rows(latent_raw[:, :KVR], latent_gain), rotate(latent_raw[:, KVR:], positions)],
        axis=-1,
    ).astype(jnp.bfloat16)
    latent_width = new_latents.shape[1]
    span_blocks = lax.axis_size("tq")
    span_rows = lax.all_to_all(
        jnp.broadcast_to(new_latents, (span_blocks,) + new_latents.shape), "tq", 0, 0, tiled=True
    ).reshape(-1, latent_width)
    span_lower = jnp.zeros((tok_dev,), jnp.int32)
    span_limit = within + 1
    group_prompts = prompt_of[group_index * group_requests + jnp.arange(group_requests)]
    prompt_send = jnp.take(prompt_latents, group_prompts, axis=0)
    prompt_rows = lax.all_to_all(
        jnp.tile(prompt_send, (span_blocks, 1, 1)), ("tq", "tr"), 0, 0, tiled=True
    ).reshape(-1, latent_width)
    cache_send, _ = lax.optimization_barrier(
        (jnp.tile(cache_latents, (span_blocks, 1, 1)), prompt_rows)
    )
    cache_rows = lax.all_to_all(cache_send, ("tq", "tr"), 0, 0, tiled=True).reshape(
        -1, latent_width
    )
    query_rows = queries.reshape(tok_dev * HEADS, latent_width)
    score_scale = 1.0 / (NOPE + ROPE) ** 0.5
    lims = jnp.stack([prompt_live, cache_live]).astype(jnp.int32)
    lim_rows = jnp.repeat(span_limit, HEADS)[:, None]
    early_state = flash_part(
        lims,
        lim_rows,
        query_rows,
        (("span", span_rows), ("prompt", prompt_rows)),
        None,
        False,
        score_scale,
        KVR,
    )
    latent_out = flash_part(
        lims, lim_rows, query_rows, (("cache", cache_rows),), early_state, True, score_scale, KVR
    ).reshape(tok_dev, HEADS, KVR)
    heads_out = (
        jnp.einsum(
            "thk,khv->thv",
            latent_out,
            value_up.reshape(KVR, HEADS, VDIM),
            preferred_element_type=jnp.float32,
        )
        .astype(jnp.bfloat16)
        .reshape(tok_dev, HEADS * VDIM)
    )
    attended = jnp.dot(heads_out, output_weight, preferred_element_type=jnp.float32)
    weights_full = lax.all_gather(
        jnp.stack([gate_weight, up_weight, down_weight.T]), ("tq", "tr"), axis=1, tiled=True
    )
    residual, weights_full = lax.optimization_barrier(
        ((tokens.astype(jnp.float32) + attended).astype(jnp.bfloat16), weights_full)
    )
    post_norm = norm_rows(residual.astype(jnp.float32), post_gain).astype(jnp.bfloat16)
    half_width = post_norm.shape[1] // 2
    group_count = lax.axis_size("grp")
    rows_all = jnp.concatenate(
        [
            lax.all_gather(post_norm[:, :half_width], "grp", axis=0, tiled=True),
            lax.all_to_all(
                jnp.broadcast_to(
                    post_norm[:, half_width:], (group_count, tok_dev, half_width)
                ),
                "grp",
                0,
                0,
                tiled=True,
            ).reshape(group_count * tok_dev, half_width),
        ],
        axis=1,
    )
    gate_full, up_full, down_full = weights_full
    gate_values = jnp.dot(rows_all, gate_full, preferred_element_type=jnp.float32)
    up_values = jnp.dot(rows_all, up_full, preferred_element_type=jnp.float32)
    hidden = (jax.nn.silu(gate_values) * up_values).astype(jnp.bfloat16)
    partial_out = lax.dot_general(
        hidden, down_full, (((1,), (1,)), ((), ())), preferred_element_type=jnp.float32
    )
    partial_out = partial_out.astype(jnp.bfloat16)
    down_values = jnp.concatenate(
        [
            lax.psum_scatter(
                partial_out[:, :half_width], "grp", scatter_dimension=0, tiled=True
            ).astype(jnp.float32),
            lax.all_to_all(
                partial_out[:, half_width:].reshape(group_count, tok_dev, half_width),
                "grp",
                0,
                0,
                tiled=True,
            )
            .astype(jnp.float32)
            .sum(axis=0),
        ],
        axis=1,
    )
    layer_out = (residual.astype(jnp.float32) + down_values).astype(jnp.bfloat16)
    return (layer_out, new_latents)


def solution(mesh):
    split = ("grp", "tq", "tr")
    tokens_spec = P(split, None)
    in_specs = (
        tokens_spec,
        P(),
        P(),
        P(),
        P(),
        P(),
        P(),
        P(),
        P(),
        P(),
        P(),
        P(("tq", "tr"), "grp"),
        P(("tq", "tr"), "grp"),
        P("grp", ("tq", "tr")),
        P("grp", ("tq", "tr"), None),
        P(None, ("tq", "tr"), None),
        P(),
        P(),
        P(),
    )
    out_specs = (tokens_spec, tokens_spec)

    def run(*args):
        n_grp, n_tok = mesh.shape["grp"], mesh.shape["tok"]
        tok_dev = args[0].shape[0] // (n_grp * n_tok)
        group_requests = tok_dev * n_tok // SPAN
        sub = Mesh(
            mesh.devices.reshape(n_grp, n_tok // group_requests, group_requests), split
        )
        return jax.shard_map(
            body, mesh=sub, in_specs=in_specs, out_specs=out_specs, check_vma=False
        )(*args)

    return run
```

```python
import jax
import jax.numpy as jnp
from jax import lax
from jax.sharding import Mesh, PartitionSpec as P
import functools
from jax.experimental import pallas as pl
from jax.experimental.pallas import tpu as pltpu

KVR = 256
HEADS = 20
NOPE = 64
ROPE = 32
VDIM = 64
SPAN = 1024


EPSILON = 1e-06


def passed_along(block, axis, distance):
    devices = range(lax.axis_size(axis))
    route = [(i - distance, i) for i in devices if i - distance in devices]
    return lax.ppermute(block, axis, route)


def norm_rows(values, gain_vector):
    mean_square = jnp.mean(values * values, axis=-1, keepdims=True)
    return values * lax.rsqrt(mean_square + EPSILON) * gain_vector.astype(jnp.float32)


def rotate(values, positions):
    half_width = values.shape[-1] // 2
    frequency = 10000.0 ** (-jnp.arange(half_width, dtype=jnp.float32) / half_width)
    angles = positions.astype(jnp.float32)[:, None] * frequency[None, :]
    if values.ndim == 3:
        angles = angles[:, None, :]
    cosine = jnp.cos(angles)
    sine_part = jnp.sin(angles)
    leading = values[..., :half_width]
    trailing = values[..., half_width:]
    return jnp.concatenate(
        [leading * cosine - trailing * sine_part, trailing * cosine + leading * sine_part], axis=-1
    )


KEY_BLOCK = 512
ROW_BLOCK = 2560


def flash_kernel(lims_ref, lim_row_ref, q_ref, *refs, plan, first, final, score_scale, value_width):
    key_refs = refs[: len(plan)]
    rest = refs[len(plan) :]
    if not first:
        m_in, l_in, acc_in = rest[:3]
        rest = rest[3:]
    if final:
        o_ref = rest[0]
        rest = rest[1:]
    else:
        m_out, l_out, acc_out = rest[:3]
        rest = rest[3:]
    m_sc, l_sc, acc_sc = rest
    j = pl.program_id(1)
    total = sum(count for _, count in plan)
    rows = q_ref.shape[0]

    @pl.when(j == 0)
    def _init():
        if first:
            m_sc[...] = jnp.full(m_sc.shape, -1e30, jnp.float32)
            l_sc[...] = jnp.zeros(l_sc.shape, jnp.float32)
            acc_sc[...] = jnp.zeros(acc_sc.shape, jnp.float32)
        else:
            m_sc[...] = m_in[...]
            l_sc[...] = l_in[...]
            acc_sc[...] = acc_in[...]

    def step(k_ref, base, limit):
        keys = k_ref[...]
        scores = lax.dot_general(q_ref[...], keys, (((1,), (1,)), ((), ())), preferred_element_type=jnp.float32) * score_scale
        place = lax.broadcasted_iota(jnp.int32, scores.shape, 1) + base
        live = place < limit
        m_old = m_sc[...]
        m_new = jnp.maximum(m_old, jnp.max(jnp.where(live, scores, -1e30), axis=1, keepdims=True))
        weights = jnp.where(live, jnp.exp(scores - m_new), 0.0)
        factor = jnp.exp(m_old - m_new)
        l_sc[...] = l_sc[...] * factor + jnp.sum(weights, axis=1, keepdims=True)
        acc_sc[...] = acc_sc[...] * factor + jnp.dot(weights.astype(jnp.bfloat16), keys[:, :value_width], preferred_element_type=jnp.float32)
        m_sc[...] = m_new

    begin = 0
    for (kind, count), k_ref in zip(plan, key_refs):
        def run(k_ref=k_ref, kind=kind, begin=begin):
            if kind == "span":
                limit = lim_row_ref[...]
            else:
                limit = jnp.full((rows, 1), lims_ref[0 if kind == "prompt" else 1], jnp.int32)
            step(k_ref, (j - begin) * KEY_BLOCK, limit)
        pl.when(jnp.logical_and(j >= begin, j < begin + count))(run)
        begin += count

    @pl.when(j == total - 1)
    def _finish():
        if final:
            o_ref[...] = (acc_sc[...] / l_sc[...]).astype(o_ref.dtype)
        else:
            m_out[...] = m_sc[...]
            l_out[...] = l_sc[...]
            acc_out[...] = acc_sc[...]


def flash_part(lims, lim_rows, queries, segments, state, final, score_scale, value_width, interpret=False):
    row_count, width = queries.shape
    plan = tuple((kind, rows.shape[0] // KEY_BLOCK) for kind, rows in segments)
    total = sum(count for _, count in plan)
    grid = (row_count // ROW_BLOCK, total)
    key_specs = []
    begin = 0
    for _, count in plan:
        key_specs.append(pl.BlockSpec((KEY_BLOCK, width), lambda i, j, lims, b=begin, c=count: (jnp.minimum(jnp.maximum(j - b, 0), c - 1), 0)))
        begin += count
    row_spec = lambda cols: pl.BlockSpec((ROW_BLOCK, cols), lambda i, j, lims: (i, 0))
    in_specs = [row_spec(1), row_spec(width)] + key_specs
    operands = [lims, lim_rows, queries] + [rows for _, rows in segments]
    if state is not None:
        in_specs += [row_spec(1), row_spec(1), row_spec(value_width)]
        operands += list(state)
    if final:
        out_specs = row_spec(value_width)
        out_shape = jax.ShapeDtypeStruct((row_count, value_width), jnp.bfloat16)
    else:
        out_specs = [row_spec(1), row_spec(1), row_spec(value_width)]
        out_shape = [
            jax.ShapeDtypeStruct((row_count, 1), jnp.float32),
            jax.ShapeDtypeStruct((row_count, 1), jnp.float32),
            jax.ShapeDtypeStruct((row_count, value_width), jnp.float32),
        ]
    key_count = total * KEY_BLOCK
    kernel = functools.partial(flash_kernel, plan=plan, first=state is None, final=final, score_scale=score_scale, value_width=value_width)
    return pl.pallas_call(
        kernel,
        grid_spec=pltpu.PrefetchScalarGridSpec(
            num_scalar_prefetch=1,
            grid=grid,
            in_specs=in_specs,
            out_specs=out_specs,
            scratch_shapes=[
                pltpu.VMEM((ROW_BLOCK, 1), jnp.float32),
                pltpu.VMEM((ROW_BLOCK, 1), jnp.float32),
                pltpu.VMEM((ROW_BLOCK, value_width), jnp.float32),
            ],
        ),
        out_shape=out_shape,
        compiler_params=pltpu.CompilerParams(dimension_semantics=("arbitrary", "arbitrary")),
        interpret=interpret,
        cost_estimate=pl.CostEstimate(
            flops=2 * row_count * key_count * (width + value_width),
            transcendentals=row_count * key_count,
            bytes_accessed=2 * (row_count * (width + value_width) + key_count * width),
        ),
    )(*operands)


def attend_segment(
    softmax_state, queries, key_rows, lowers, limits, block_count, key_block, score_scale
):

    def fold_block(step_index, carried):
        running_max, running_sum, running_out = carried
        first_key = step_index * key_block
        key_piece = lax.dynamic_slice_in_dim(key_rows, first_key, key_block, 0)
        scores = (
            jnp.einsum("rw,kw->rk", queries, key_piece, preferred_element_type=jnp.float32)
            * score_scale
        )
        key_place = (first_key + jnp.arange(key_block, dtype=jnp.int32))[None, :]
        live_keys = jnp.logical_and(key_place >= lowers[:, None], key_place < limits[:, None])
        next_max = jnp.maximum(running_max, jnp.max(jnp.where(live_keys, scores, -1e30), axis=1))
        weights = jnp.where(live_keys, jnp.exp(scores - next_max[:, None]), 0.0)
        factor = jnp.exp(running_max - next_max)
        running_sum = running_sum * factor + jnp.sum(weights, axis=1)
        running_out = running_out * factor[:, None] + jnp.dot(
            weights.astype(jnp.bfloat16), key_piece[:, :KVR], preferred_element_type=jnp.float32
        )
        return (next_max, running_sum, running_out)

    return lax.fori_loop(0, block_count, fold_block, softmax_state)


def body(
    tokens,
    input_gain,
    query_down,
    query_gain,
    query_up,
    latent_down,
    latent_gain,
    key_up,
    value_up,
    output_weight,
    post_gain,
    gate_weight,
    up_weight,
    down_weight,
    cache_latents,
    prompt_latents,
    cache_len,
    prompt_len,
    prompt_of,
):
    group_index = lax.axis_index("grp")
    span_index = lax.axis_index("tq")
    local_request = lax.axis_index("tr")
    tok_dev = tokens.shape[0]
    group_requests = lax.axis_size("tr")
    owner = group_index * group_requests + local_request
    offset = span_index * tok_dev
    within = offset + jnp.arange(tok_dev, dtype=jnp.int32)
    own_prompt = prompt_of[owner]
    prompt_live = prompt_len[own_prompt]
    cache_live = cache_len[owner]
    positions = prompt_live + cache_live + within
    normed = norm_rows(tokens.astype(jnp.float32), input_gain).astype(jnp.bfloat16)
    query_latent = norm_rows(
        jnp.dot(normed, query_down, preferred_element_type=jnp.float32), query_gain
    ).astype(jnp.bfloat16)
    query_full = jnp.dot(query_latent, query_up, preferred_element_type=jnp.float32).astype(
        jnp.bfloat16
    )
    query_full = lax.optimization_barrier(query_full).reshape(tok_dev, HEADS, NOPE + ROPE)
    absorbed = jnp.einsum(
        "thd,khd->thk",
        query_full[..., :NOPE],
        key_up.reshape(KVR, HEADS, NOPE),
        preferred_element_type=jnp.float32,
    )
    turned = rotate(query_full[..., NOPE:].astype(jnp.float32), positions)
    queries = jnp.concatenate([absorbed, turned], axis=-1).astype(jnp.bfloat16)
    latent_raw = jnp.dot(normed, latent_down, preferred_element_type=jnp.float32)
    new_latents = jnp.concatenate(
        [norm_rows(latent_raw[:, :KVR], latent_gain), rotate(latent_raw[:, KVR:], positions)],
        axis=-1,
    ).astype(jnp.bfloat16)
    latent_width = new_latents.shape[1]
    span_blocks = lax.axis_size("tq")
    span_rows = lax.all_to_all(
        jnp.broadcast_to(new_latents, (span_blocks,) + new_latents.shape), "tq", 0, 0, tiled=True
    ).reshape(-1, latent_width)
    span_lower = jnp.zeros((tok_dev,), jnp.int32)
    span_limit = within + 1
    group_prompts = prompt_of[group_index * group_requests + jnp.arange(group_requests)]
    prompt_send = jnp.take(prompt_latents, group_prompts, axis=0)
    prompt_rows = lax.all_to_all(
        jnp.tile(prompt_send, (span_blocks, 1, 1)), ("tq", "tr"), 0, 0, tiled=True
    ).reshape(-1, latent_width)
    cache_send, _ = lax.optimization_barrier(
        (jnp.tile(cache_latents, (span_blocks, 1, 1)), prompt_rows)
    )
    cache_rows = lax.all_to_all(cache_send, ("tq", "tr"), 0, 0, tiled=True).reshape(
        -1, latent_width
    )
    query_rows = queries.reshape(tok_dev * HEADS, latent_width)
    score_scale = 1.0 / (NOPE + ROPE) ** 0.5
    lims = jnp.stack([prompt_live, cache_live]).astype(jnp.int32)
    lim_rows = jnp.repeat(span_limit, HEADS)[:, None]
    early_state = flash_part(
        lims,
        lim_rows,
        query_rows,
        (("span", span_rows), ("prompt", prompt_rows)),
        None,
        False,
        score_scale,
        KVR,
    )
    latent_out = flash_part(
        lims, lim_rows, query_rows, (("cache", cache_rows),), early_state, True, score_scale, KVR
    ).reshape(tok_dev, HEADS, KVR)
    heads_out = (
        jnp.einsum(
            "thk,khv->thv",
            latent_out,
            value_up.reshape(KVR, HEADS, VDIM),
            preferred_element_type=jnp.float32,
        )
        .astype(jnp.bfloat16)
        .reshape(tok_dev, HEADS * VDIM)
    )
    attended = jnp.dot(heads_out, output_weight, preferred_element_type=jnp.float32)
    weights_full = lax.all_gather(
        jnp.stack([gate_weight, up_weight, down_weight.T]), ("tq", "tr"), axis=1, tiled=True
    )
    residual, weights_full = lax.optimization_barrier(
        ((tokens.astype(jnp.float32) + attended).astype(jnp.bfloat16), weights_full)
    )
    post_norm = norm_rows(residual.astype(jnp.float32), post_gain).astype(jnp.bfloat16)
    half_width = post_norm.shape[1] // 2
    group_count = lax.axis_size("grp")
    rows_all = jnp.concatenate(
        [
            lax.all_gather(post_norm[:, :half_width], "grp", axis=0, tiled=True),
            lax.all_to_all(
                jnp.broadcast_to(
                    post_norm[:, half_width:], (group_count, tok_dev, half_width)
                ),
                "grp",
                0,
                0,
                tiled=True,
            ).reshape(group_count * tok_dev, half_width),
        ],
        axis=1,
    )
    gate_full, up_full, down_full = weights_full
    gate_values = jnp.dot(rows_all, gate_full, preferred_element_type=jnp.float32)
    up_values = jnp.dot(rows_all, up_full, preferred_element_type=jnp.float32)
    hidden = (jax.nn.silu(gate_values) * up_values).astype(jnp.bfloat16)
    partial_out = lax.dot_general(
        hidden, down_full, (((1,), (1,)), ((), ())), preferred_element_type=jnp.float32
    )
    partial_out = partial_out.astype(jnp.bfloat16)
    down_values = jnp.concatenate(
        [
            lax.psum_scatter(
                partial_out[:, :half_width], "grp", scatter_dimension=0, tiled=True
            ).astype(jnp.float32),
            lax.all_to_all(
                partial_out[:, half_width:].reshape(group_count, tok_dev, half_width),
                "grp",
                0,
                0,
                tiled=True,
            )
            .astype(jnp.float32)
            .sum(axis=0),
        ],
        axis=1,
    )
    layer_out = (residual.astype(jnp.float32) + down_values).astype(jnp.bfloat16)
    return (layer_out, new_latents)


def solution(mesh):
    split = ("grp", "tq", "tr")
    tokens_spec = P(split, None)
    in_specs = (
        tokens_spec,
        P(),
        P(),
        P(),
        P(),
        P(),
        P(),
        P(),
        P(),
        P(),
        P(),
        P(("tq", "tr"), "grp"),
        P(("tq", "tr"), "grp"),
        P("grp", ("tq", "tr")),
        P("grp", ("tq", "tr"), None),
        P(None, ("tq", "tr"), None),
        P(),
        P(),
        P(),
    )
    out_specs = (tokens_spec, tokens_spec)

    def run(*args):
        n_grp, n_tok = mesh.shape["grp"], mesh.shape["tok"]
        tok_dev = args[0].shape[0] // (n_grp * n_tok)
        group_requests = tok_dev * n_tok // SPAN
        sub = Mesh(
            mesh.devices.reshape(n_grp, n_tok // group_requests, group_requests), split
        )
        return jax.shard_map(
            body, mesh=sub, in_specs=in_specs, out_specs=out_specs, check_vma=False
        )(*args)

    return run
```

```python
import jax
import jax.numpy as jnp
from jax import lax
from jax.sharding import Mesh, PartitionSpec as P
import functools
from jax.experimental import pallas as pl
from jax.experimental.pallas import tpu as pltpu

KVR = 256
HEADS = 20
NOPE = 64
ROPE = 32
VDIM = 64
SPAN = 1024


EPSILON = 1e-06


def passed_along(block, axis, distance):
    devices = range(lax.axis_size(axis))
    route = [(i - distance, i) for i in devices if i - distance in devices]
    return lax.ppermute(block, axis, route)


def norm_rows(values, gain_vector):
    mean_square = jnp.mean(values * values, axis=-1, keepdims=True)
    return values * lax.rsqrt(mean_square + EPSILON) * gain_vector.astype(jnp.float32)


def rotate(values, positions):
    half_width = values.shape[-1] // 2
    frequency = 10000.0 ** (-jnp.arange(half_width, dtype=jnp.float32) / half_width)
    angles = positions.astype(jnp.float32)[:, None] * frequency[None, :]
    if values.ndim == 3:
        angles = angles[:, None, :]
    cosine = jnp.cos(angles)
    sine_part = jnp.sin(angles)
    leading = values[..., :half_width]
    trailing = values[..., half_width:]
    return jnp.concatenate(
        [leading * cosine - trailing * sine_part, trailing * cosine + leading * sine_part], axis=-1
    )


KEY_BLOCK = 1024
ROW_BLOCK = 1280


def flash_kernel(lims_ref, lim_row_ref, q_ref, *refs, plan, first, final, score_scale, value_width):
    key_refs = refs[: len(plan)]
    rest = refs[len(plan) :]
    if not first:
        m_in, l_in, acc_in = rest[:3]
        rest = rest[3:]
    if final:
        o_ref = rest[0]
        rest = rest[1:]
    else:
        m_out, l_out, acc_out = rest[:3]
        rest = rest[3:]
    m_sc, l_sc, acc_sc = rest
    j = pl.program_id(1)
    total = sum(count for _, count in plan)
    rows = q_ref.shape[0]

    @pl.when(j == 0)
    def _init():
        if first:
            m_sc[...] = jnp.full(m_sc.shape, -1e30, jnp.float32)
            l_sc[...] = jnp.zeros(l_sc.shape, jnp.float32)
            acc_sc[...] = jnp.zeros(acc_sc.shape, jnp.float32)
        else:
            m_sc[...] = m_in[...]
            l_sc[...] = l_in[...]
            acc_sc[...] = acc_in[...]

    def step(k_ref, base, limit):
        keys = k_ref[...]
        scores = lax.dot_general(q_ref[...], keys, (((1,), (1,)), ((), ())), preferred_element_type=jnp.float32) * score_scale
        place = lax.broadcasted_iota(jnp.int32, scores.shape, 1) + base
        live = place < limit
        m_old = m_sc[...]
        m_new = jnp.maximum(m_old, jnp.max(jnp.where(live, scores, -1e30), axis=1, keepdims=True))
        weights = jnp.where(live, jnp.exp(scores - m_new), 0.0)
        factor = jnp.exp(m_old - m_new)
        l_sc[...] = l_sc[...] * factor + jnp.sum(weights, axis=1, keepdims=True)
        acc_sc[...] = acc_sc[...] * factor + jnp.dot(weights.astype(jnp.bfloat16), keys[:, :value_width], preferred_element_type=jnp.float32)
        m_sc[...] = m_new

    begin = 0
    for (kind, count), k_ref in zip(plan, key_refs):
        def run(k_ref=k_ref, kind=kind, begin=begin):
            if kind == "span":
                limit = lim_row_ref[...]
            else:
                limit = jnp.full((rows, 1), lims_ref[0 if kind == "prompt" else 1], jnp.int32)
            step(k_ref, (j - begin) * KEY_BLOCK, limit)
        pl.when(jnp.logical_and(j >= begin, j < begin + count))(run)
        begin += count

    @pl.when(j == total - 1)
    def _finish():
        if final:
            o_ref[...] = (acc_sc[...] / l_sc[...]).astype(o_ref.dtype)
        else:
            m_out[...] = m_sc[...]
            l_out[...] = l_sc[...]
            acc_out[...] = acc_sc[...]


def flash_part(lims, lim_rows, queries, segments, state, final, score_scale, value_width, interpret=False):
    row_count, width = queries.shape
    plan = tuple((kind, rows.shape[0] // KEY_BLOCK) for kind, rows in segments)
    total = sum(count for _, count in plan)
    grid = (row_count // ROW_BLOCK, total)
    key_specs = []
    begin = 0
    for _, count in plan:
        key_specs.append(pl.BlockSpec((KEY_BLOCK, width), lambda i, j, lims, b=begin, c=count: (jnp.minimum(jnp.maximum(j - b, 0), c - 1), 0)))
        begin += count
    row_spec = lambda cols: pl.BlockSpec((ROW_BLOCK, cols), lambda i, j, lims: (i, 0))
    in_specs = [row_spec(1), row_spec(width)] + key_specs
    operands = [lims, lim_rows, queries] + [rows for _, rows in segments]
    if state is not None:
        in_specs += [row_spec(1), row_spec(1), row_spec(value_width)]
        operands += list(state)
    if final:
        out_specs = row_spec(value_width)
        out_shape = jax.ShapeDtypeStruct((row_count, value_width), jnp.bfloat16)
    else:
        out_specs = [row_spec(1), row_spec(1), row_spec(value_width)]
        out_shape = [
            jax.ShapeDtypeStruct((row_count, 1), jnp.float32),
            jax.ShapeDtypeStruct((row_count, 1), jnp.float32),
            jax.ShapeDtypeStruct((row_count, value_width), jnp.float32),
        ]
    key_count = total * KEY_BLOCK
    kernel = functools.partial(flash_kernel, plan=plan, first=state is None, final=final, score_scale=score_scale, value_width=value_width)
    return pl.pallas_call(
        kernel,
        grid_spec=pltpu.PrefetchScalarGridSpec(
            num_scalar_prefetch=1,
            grid=grid,
            in_specs=in_specs,
            out_specs=out_specs,
            scratch_shapes=[
                pltpu.VMEM((ROW_BLOCK, 1), jnp.float32),
                pltpu.VMEM((ROW_BLOCK, 1), jnp.float32),
                pltpu.VMEM((ROW_BLOCK, value_width), jnp.float32),
            ],
        ),
        out_shape=out_shape,
        compiler_params=pltpu.CompilerParams(dimension_semantics=("arbitrary", "arbitrary")),
        interpret=interpret,
        cost_estimate=pl.CostEstimate(
            flops=2 * row_count * key_count * (width + value_width),
            transcendentals=row_count * key_count,
            bytes_accessed=2 * (row_count * (width + value_width) + key_count * width),
        ),
    )(*operands)


def attend_segment(
    softmax_state, queries, key_rows, lowers, limits, block_count, key_block, score_scale
):

    def fold_block(step_index, carried):
        running_max, running_sum, running_out = carried
        first_key = step_index * key_block
        key_piece = lax.dynamic_slice_in_dim(key_rows, first_key, key_block, 0)
        scores = (
            jnp.einsum("rw,kw->rk", queries, key_piece, preferred_element_type=jnp.float32)
            * score_scale
        )
        key_place = (first_key + jnp.arange(key_block, dtype=jnp.int32))[None, :]
        live_keys = jnp.logical_and(key_place >= lowers[:, None], key_place < limits[:, None])
        next_max = jnp.maximum(running_max, jnp.max(jnp.where(live_keys, scores, -1e30), axis=1))
        weights = jnp.where(live_keys, jnp.exp(scores - next_max[:, None]), 0.0)
        factor = jnp.exp(running_max - next_max)
        running_sum = running_sum * factor + jnp.sum(weights, axis=1)
        running_out = running_out * factor[:, None] + jnp.dot(
            weights.astype(jnp.bfloat16), key_piece[:, :KVR], preferred_element_type=jnp.float32
        )
        return (next_max, running_sum, running_out)

    return lax.fori_loop(0, block_count, fold_block, softmax_state)


def body(
    tokens,
    input_gain,
    query_down,
    query_gain,
    query_up,
    latent_down,
    latent_gain,
    key_up,
    value_up,
    output_weight,
    post_gain,
    gate_weight,
    up_weight,
    down_weight,
    cache_latents,
    prompt_latents,
    cache_len,
    prompt_len,
    prompt_of,
):
    group_index = lax.axis_index("grp")
    span_index = lax.axis_index("tq")
    local_request = lax.axis_index("tr")
    tok_dev = tokens.shape[0]
    group_requests = lax.axis_size("tr")
    owner = group_index * group_requests + local_request
    offset = span_index * tok_dev
    within = offset + jnp.arange(tok_dev, dtype=jnp.int32)
    own_prompt = prompt_of[owner]
    prompt_live = prompt_len[own_prompt]
    cache_live = cache_len[owner]
    positions = prompt_live + cache_live + within
    normed = norm_rows(tokens.astype(jnp.float32), input_gain).astype(jnp.bfloat16)
    query_latent = norm_rows(
        jnp.dot(normed, query_down, preferred_element_type=jnp.float32), query_gain
    ).astype(jnp.bfloat16)
    query_full = jnp.dot(query_latent, query_up, preferred_element_type=jnp.float32).astype(
        jnp.bfloat16
    )
    query_full = lax.optimization_barrier(query_full).reshape(tok_dev, HEADS, NOPE + ROPE)
    absorbed = jnp.einsum(
        "thd,khd->thk",
        query_full[..., :NOPE],
        key_up.reshape(KVR, HEADS, NOPE),
        preferred_element_type=jnp.float32,
    )
    turned = rotate(query_full[..., NOPE:].astype(jnp.float32), positions)
    queries = jnp.concatenate([absorbed, turned], axis=-1).astype(jnp.bfloat16)
    latent_raw = jnp.dot(normed, latent_down, preferred_element_type=jnp.float32)
    new_latents = jnp.concatenate(
        [norm_rows(latent_raw[:, :KVR], latent_gain), rotate(latent_raw[:, KVR:], positions)],
        axis=-1,
    ).astype(jnp.bfloat16)
    latent_width = new_latents.shape[1]
    span_blocks = lax.axis_size("tq")

    span_lower = jnp.zeros((tok_dev,), jnp.int32)
    span_limit = within + 1
    group_prompts = prompt_of[group_index * group_requests + jnp.arange(group_requests)]
    prompt_send = jnp.take(prompt_latents, group_prompts, axis=0)
    cache_rows = lax.all_to_all(
        jnp.tile(cache_latents, (span_blocks, 1, 1)), ("tq", "tr"), 0, 0, tiled=True
    ).reshape(-1, latent_width)
    tok_slots = span_blocks * group_requests
    mates = (jnp.arange(tok_slots) % group_requests == local_request)[:, None, None]
    span_send = jnp.where(
        mates, jnp.broadcast_to(new_latents, (tok_slots,) + new_latents.shape), 0
    ).astype(new_latents.dtype)
    late_send, _ = lax.optimization_barrier(
        (jnp.concatenate([jnp.tile(prompt_send, (span_blocks, 1, 1)), span_send], axis=1), cache_rows)
    )
    late_rows = lax.all_to_all(late_send, ("tq", "tr"), 0, 0, tiled=True)
    prompt_piece = prompt_send.shape[1]
    prompt_rows = late_rows[:, :prompt_piece].reshape(-1, latent_width)
    span_rows = (
        late_rows[:, prompt_piece:]
        .reshape(span_blocks, group_requests, tok_dev, latent_width)
        .take(local_request, axis=1)
        .reshape(-1, latent_width)
    )
    query_rows = queries.reshape(tok_dev * HEADS, latent_width)
    score_scale = 1.0 / (NOPE + ROPE) ** 0.5
    lims = jnp.stack([prompt_live, cache_live]).astype(jnp.int32)
    lim_rows = jnp.repeat(span_limit, HEADS)[:, None]
    early_state = flash_part(
        lims, lim_rows, query_rows, (("cache", cache_rows),), None, False, score_scale, KVR
    )
    latent_out = flash_part(
        lims,
        lim_rows,
        query_rows,
        (("span", span_rows), ("prompt", prompt_rows)),
        early_state,
        True,
        score_scale,
        KVR,
    ).reshape(tok_dev, HEADS, KVR)
    heads_out = (
        jnp.einsum(
            "thk,khv->thv",
            latent_out,
            value_up.reshape(KVR, HEADS, VDIM),
            preferred_element_type=jnp.float32,
        )
        .astype(jnp.bfloat16)
        .reshape(tok_dev, HEADS * VDIM)
    )
    attended = jnp.dot(heads_out, output_weight, preferred_element_type=jnp.float32)
    weights_full = lax.all_gather(
        jnp.stack([gate_weight, up_weight, down_weight.T]), ("tq", "tr"), axis=1, tiled=True
    )
    residual, weights_full = lax.optimization_barrier(
        ((tokens.astype(jnp.float32) + attended).astype(jnp.bfloat16), weights_full)
    )
    post_norm = norm_rows(residual.astype(jnp.float32), post_gain).astype(jnp.bfloat16)
    half_width = post_norm.shape[1] // 2
    group_count = lax.axis_size("grp")
    rows_all = jnp.concatenate(
        [
            lax.all_gather(post_norm[:, :half_width], "grp", axis=0, tiled=True),
            lax.all_to_all(
                jnp.broadcast_to(
                    post_norm[:, half_width:], (group_count, tok_dev, half_width)
                ),
                "grp",
                0,
                0,
                tiled=True,
            ).reshape(group_count * tok_dev, half_width),
        ],
        axis=1,
    )
    gate_full, up_full, down_full = weights_full
    gate_values = jnp.dot(rows_all, gate_full, preferred_element_type=jnp.float32)
    up_values = jnp.dot(rows_all, up_full, preferred_element_type=jnp.float32)
    hidden = (jax.nn.silu(gate_values) * up_values).astype(jnp.bfloat16)
    partial_out = lax.dot_general(
        hidden, down_full, (((1,), (1,)), ((), ())), preferred_element_type=jnp.float32
    )
    partial_out = partial_out.astype(jnp.bfloat16)
    down_values = jnp.concatenate(
        [
            lax.psum_scatter(
                partial_out[:, :half_width], "grp", scatter_dimension=0, tiled=True
            ).astype(jnp.float32),
            lax.all_to_all(
                partial_out[:, half_width:].reshape(group_count, tok_dev, half_width),
                "grp",
                0,
                0,
                tiled=True,
            )
            .astype(jnp.float32)
            .sum(axis=0),
        ],
        axis=1,
    )
    layer_out = (residual.astype(jnp.float32) + down_values).astype(jnp.bfloat16)
    return (layer_out, new_latents)


def solution(mesh):
    split = ("grp", "tq", "tr")
    tokens_spec = P(split, None)
    in_specs = (
        tokens_spec,
        P(),
        P(),
        P(),
        P(),
        P(),
        P(),
        P(),
        P(),
        P(),
        P(),
        P(("tq", "tr"), "grp"),
        P(("tq", "tr"), "grp"),
        P("grp", ("tq", "tr")),
        P("grp", ("tq", "tr"), None),
        P(None, ("tq", "tr"), None),
        P(),
        P(),
        P(),
    )
    out_specs = (tokens_spec, tokens_spec)

    def run(*args):
        n_grp, n_tok = mesh.shape["grp"], mesh.shape["tok"]
        tok_dev = args[0].shape[0] // (n_grp * n_tok)
        group_requests = tok_dev * n_tok // SPAN
        sub = Mesh(
            mesh.devices.reshape(n_grp, n_tok // group_requests, group_requests), split
        )
        return jax.shard_map(
            body, mesh=sub, in_specs=in_specs, out_specs=out_specs, check_vma=False
        )(*args)

    return run
```

```python
import jax
import jax.numpy as jnp
from jax import lax
from jax.sharding import Mesh, PartitionSpec as P
import functools
from jax.experimental import pallas as pl
from jax.experimental.pallas import tpu as pltpu

KVR = 256
HEADS = 20
NOPE = 64
ROPE = 32
VDIM = 64
SPAN = 1024


EPSILON = 1e-06


def passed_along(block, axis, distance):
    devices = range(lax.axis_size(axis))
    route = [(i - distance, i) for i in devices if i - distance in devices]
    return lax.ppermute(block, axis, route)


def norm_rows(values, gain_vector):
    mean_square = jnp.mean(values * values, axis=-1, keepdims=True)
    return values * lax.rsqrt(mean_square + EPSILON) * gain_vector.astype(jnp.float32)


def rotate(values, positions):
    half_width = values.shape[-1] // 2
    frequency = 10000.0 ** (-jnp.arange(half_width, dtype=jnp.float32) / half_width)
    angles = positions.astype(jnp.float32)[:, None] * frequency[None, :]
    if values.ndim == 3:
        angles = angles[:, None, :]
    cosine = jnp.cos(angles)
    sine_part = jnp.sin(angles)
    leading = values[..., :half_width]
    trailing = values[..., half_width:]
    return jnp.concatenate(
        [leading * cosine - trailing * sine_part, trailing * cosine + leading * sine_part], axis=-1
    )


KEY_BLOCK = 1024
ROW_BLOCK = 1280


def flash_kernel(lims_ref, lim_row_ref, q_ref, *refs, plan, first, final, score_scale, value_width):
    key_refs = refs[: len(plan)]
    rest = refs[len(plan) :]
    if not first:
        m_in, l_in, acc_in = rest[:3]
        rest = rest[3:]
    if final:
        o_ref = rest[0]
        rest = rest[1:]
    else:
        m_out, l_out, acc_out = rest[:3]
        rest = rest[3:]
    m_sc, l_sc, acc_sc = rest
    j = pl.program_id(1)
    total = sum(count for _, count in plan)
    rows = q_ref.shape[0]

    @pl.when(j == 0)
    def _init():
        if first:
            m_sc[...] = jnp.full(m_sc.shape, -1e30, jnp.float32)
            l_sc[...] = jnp.zeros(l_sc.shape, jnp.float32)
            acc_sc[...] = jnp.zeros(acc_sc.shape, jnp.float32)
        else:
            m_sc[...] = m_in[...]
            l_sc[...] = l_in[...]
            acc_sc[...] = acc_in[...]

    def step(k_ref, base, limit):
        keys = k_ref[...]
        scores = lax.dot_general(q_ref[...], keys, (((1,), (1,)), ((), ())), preferred_element_type=jnp.float32) * score_scale
        place = lax.broadcasted_iota(jnp.int32, scores.shape, 1) + base
        live = place < limit
        m_old = m_sc[...]
        m_new = jnp.maximum(m_old, jnp.max(jnp.where(live, scores, -1e30), axis=1, keepdims=True))
        weights = jnp.where(live, jnp.exp(scores - m_new), 0.0)
        factor = jnp.exp(m_old - m_new)
        l_sc[...] = l_sc[...] * factor + jnp.sum(weights, axis=1, keepdims=True)
        acc_sc[...] = acc_sc[...] * factor + jnp.dot(weights.astype(jnp.bfloat16), keys[:, :value_width], preferred_element_type=jnp.float32)
        m_sc[...] = m_new

    begin = 0
    for (kind, count), k_ref in zip(plan, key_refs):
        def run(k_ref=k_ref, kind=kind, begin=begin):
            if kind == "span":
                limit = lim_row_ref[...]
            else:
                limit = jnp.full((rows, 1), lims_ref[0 if kind == "prompt" else 1], jnp.int32)
            step(k_ref, (j - begin) * KEY_BLOCK, limit)
        pl.when(jnp.logical_and(j >= begin, j < begin + count))(run)
        begin += count

    @pl.when(j == total - 1)
    def _finish():
        if final:
            o_ref[...] = (acc_sc[...] / l_sc[...]).astype(o_ref.dtype)
        else:
            m_out[...] = m_sc[...]
            l_out[...] = l_sc[...]
            acc_out[...] = acc_sc[...]


def flash_part(lims, lim_rows, queries, segments, state, final, score_scale, value_width, interpret=False):
    row_count, width = queries.shape
    plan = tuple((kind, rows.shape[0] // KEY_BLOCK) for kind, rows in segments)
    total = sum(count for _, count in plan)
    grid = (row_count // ROW_BLOCK, total)
    key_specs = []
    begin = 0
    for _, count in plan:
        key_specs.append(pl.BlockSpec((KEY_BLOCK, width), lambda i, j, lims, b=begin, c=count: (jnp.minimum(jnp.maximum(j - b, 0), c - 1), 0)))
        begin += count
    row_spec = lambda cols: pl.BlockSpec((ROW_BLOCK, cols), lambda i, j, lims: (i, 0))
    in_specs = [row_spec(1), row_spec(width)] + key_specs
    operands = [lims, lim_rows, queries] + [rows for _, rows in segments]
    if state is not None:
        in_specs += [row_spec(1), row_spec(1), row_spec(value_width)]
        operands += list(state)
    if final:
        out_specs = row_spec(value_width)
        out_shape = jax.ShapeDtypeStruct((row_count, value_width), jnp.bfloat16)
    else:
        out_specs = [row_spec(1), row_spec(1), row_spec(value_width)]
        out_shape = [
            jax.ShapeDtypeStruct((row_count, 1), jnp.float32),
            jax.ShapeDtypeStruct((row_count, 1), jnp.float32),
            jax.ShapeDtypeStruct((row_count, value_width), jnp.float32),
        ]
    key_count = total * KEY_BLOCK
    kernel = functools.partial(flash_kernel, plan=plan, first=state is None, final=final, score_scale=score_scale, value_width=value_width)
    return pl.pallas_call(
        kernel,
        grid_spec=pltpu.PrefetchScalarGridSpec(
            num_scalar_prefetch=1,
            grid=grid,
            in_specs=in_specs,
            out_specs=out_specs,
            scratch_shapes=[
                pltpu.VMEM((ROW_BLOCK, 1), jnp.float32),
                pltpu.VMEM((ROW_BLOCK, 1), jnp.float32),
                pltpu.VMEM((ROW_BLOCK, value_width), jnp.float32),
            ],
        ),
        out_shape=out_shape,
        compiler_params=pltpu.CompilerParams(dimension_semantics=("arbitrary", "arbitrary")),
        interpret=interpret,
        cost_estimate=pl.CostEstimate(
            flops=2 * row_count * key_count * (width + value_width),
            transcendentals=row_count * key_count,
            bytes_accessed=2 * (row_count * (width + value_width) + key_count * width),
        ),
    )(*operands)


def attend_segment(
    softmax_state, queries, key_rows, lowers, limits, block_count, key_block, score_scale
):

    def fold_block(step_index, carried):
        running_max, running_sum, running_out = carried
        first_key = step_index * key_block
        key_piece = lax.dynamic_slice_in_dim(key_rows, first_key, key_block, 0)
        scores = (
            jnp.einsum("rw,kw->rk", queries, key_piece, preferred_element_type=jnp.float32)
            * score_scale
        )
        key_place = (first_key + jnp.arange(key_block, dtype=jnp.int32))[None, :]
        live_keys = jnp.logical_and(key_place >= lowers[:, None], key_place < limits[:, None])
        next_max = jnp.maximum(running_max, jnp.max(jnp.where(live_keys, scores, -1e30), axis=1))
        weights = jnp.where(live_keys, jnp.exp(scores - next_max[:, None]), 0.0)
        factor = jnp.exp(running_max - next_max)
        running_sum = running_sum * factor + jnp.sum(weights, axis=1)
        running_out = running_out * factor[:, None] + jnp.dot(
            weights.astype(jnp.bfloat16), key_piece[:, :KVR], preferred_element_type=jnp.float32
        )
        return (next_max, running_sum, running_out)

    return lax.fori_loop(0, block_count, fold_block, softmax_state)


def body(
    tokens,
    input_gain,
    query_down,
    query_gain,
    query_up,
    latent_down,
    latent_gain,
    key_up,
    value_up,
    output_weight,
    post_gain,
    gate_weight,
    up_weight,
    down_weight,
    cache_latents,
    prompt_latents,
    cache_len,
    prompt_len,
    prompt_of,
):
    group_index = lax.axis_index("grp")
    span_index = lax.axis_index("tq")
    local_request = lax.axis_index("tr")
    tok_dev = tokens.shape[0]
    group_requests = lax.axis_size("tr")
    owner = group_index * group_requests + local_request
    offset = span_index * tok_dev
    within = offset + jnp.arange(tok_dev, dtype=jnp.int32)
    own_prompt = prompt_of[owner]
    prompt_live = prompt_len[own_prompt]
    cache_live = cache_len[owner]
    positions = prompt_live + cache_live + within
    normed = norm_rows(tokens.astype(jnp.float32), input_gain).astype(jnp.bfloat16)
    query_latent = norm_rows(
        jnp.dot(normed, query_down, preferred_element_type=jnp.float32), query_gain
    ).astype(jnp.bfloat16)
    query_full = jnp.dot(query_latent, query_up, preferred_element_type=jnp.float32).astype(
        jnp.bfloat16
    )
    query_full = lax.optimization_barrier(query_full).reshape(tok_dev, HEADS, NOPE + ROPE)
    absorbed = jnp.einsum(
        "thd,khd->thk",
        query_full[..., :NOPE],
        key_up.reshape(KVR, HEADS, NOPE),
        preferred_element_type=jnp.float32,
    )
    turned = rotate(query_full[..., NOPE:].astype(jnp.float32), positions)
    queries = jnp.concatenate([absorbed, turned], axis=-1).astype(jnp.bfloat16)
    latent_raw = jnp.dot(normed, latent_down, preferred_element_type=jnp.float32)
    new_latents = jnp.concatenate(
        [norm_rows(latent_raw[:, :KVR], latent_gain), rotate(latent_raw[:, KVR:], positions)],
        axis=-1,
    ).astype(jnp.bfloat16)
    latent_width = new_latents.shape[1]
    span_blocks = lax.axis_size("tq")
    span_rows = lax.all_to_all(
        jnp.broadcast_to(new_latents, (span_blocks,) + new_latents.shape), "tq", 0, 0, tiled=True
    ).reshape(-1, latent_width)
    span_lower = jnp.zeros((tok_dev,), jnp.int32)
    span_limit = within + 1
    group_prompts = prompt_of[group_index * group_requests + jnp.arange(group_requests)]
    prompt_send = jnp.take(prompt_latents, group_prompts, axis=0)
    cache_rows = lax.all_to_all(
        jnp.tile(cache_latents, (span_blocks, 1, 1)), ("tq", "tr"), 0, 0, tiled=True
    ).reshape(-1, latent_width)
    prompt_send, _ = lax.optimization_barrier(
        (jnp.tile(prompt_send, (span_blocks, 1, 1)), cache_rows)
    )
    prompt_rows = lax.all_to_all(prompt_send, ("tq", "tr"), 0, 0, tiled=True).reshape(
        -1, latent_width
    )
    query_rows = queries.reshape(tok_dev * HEADS, latent_width)
    score_scale = 1.0 / (NOPE + ROPE) ** 0.5
    lims = jnp.stack([prompt_live, cache_live]).astype(jnp.int32)
    lim_rows = jnp.repeat(span_limit, HEADS)[:, None]
    early_state = flash_part(
        lims, lim_rows, query_rows, (("cache", cache_rows),), None, False, score_scale, KVR
    )
    latent_out = flash_part(
        lims,
        lim_rows,
        query_rows,
        (("span", span_rows), ("prompt", prompt_rows)),
        early_state,
        True,
        score_scale,
        KVR,
    ).reshape(tok_dev, HEADS, KVR)
    heads_out = (
        jnp.einsum(
            "thk,khv->thv",
            latent_out,
            value_up.reshape(KVR, HEADS, VDIM),
            preferred_element_type=jnp.float32,
        )
        .astype(jnp.bfloat16)
        .reshape(tok_dev, HEADS * VDIM)
    )
    attended = jnp.dot(heads_out, output_weight, preferred_element_type=jnp.float32)
    weights_full = lax.all_gather(
        jnp.stack([gate_weight, up_weight, down_weight.T]), ("tq", "tr"), axis=1, tiled=True
    )
    residual, weights_full = lax.optimization_barrier(
        ((tokens.astype(jnp.float32) + attended).astype(jnp.bfloat16), weights_full)
    )
    post_norm = norm_rows(residual.astype(jnp.float32), post_gain).astype(jnp.bfloat16)
    half_width = post_norm.shape[1] // 2
    group_count = lax.axis_size("grp")
    rows_all = jnp.concatenate(
        [
            lax.all_gather(post_norm[:, :half_width], "grp", axis=0, tiled=True),
            lax.all_to_all(
                jnp.broadcast_to(
                    post_norm[:, half_width:], (group_count, tok_dev, half_width)
                ),
                "grp",
                0,
                0,
                tiled=True,
            ).reshape(group_count * tok_dev, half_width),
        ],
        axis=1,
    )
    gate_full, up_full, down_full = weights_full
    gate_values = jnp.dot(rows_all, gate_full, preferred_element_type=jnp.float32)
    up_values = jnp.dot(rows_all, up_full, preferred_element_type=jnp.float32)
    hidden = (jax.nn.silu(gate_values) * up_values).astype(jnp.bfloat16)
    partial_out = lax.dot_general(
        hidden, down_full, (((1,), (1,)), ((), ())), preferred_element_type=jnp.float32
    )
    partial_out = partial_out.astype(jnp.bfloat16)
    down_values = jnp.concatenate(
        [
            lax.psum_scatter(
                partial_out[:, :half_width], "grp", scatter_dimension=0, tiled=True
            ).astype(jnp.float32),
            lax.all_to_all(
                partial_out[:, half_width:].reshape(group_count, tok_dev, half_width),
                "grp",
                0,
                0,
                tiled=True,
            )
            .astype(jnp.float32)
            .sum(axis=0),
        ],
        axis=1,
    )
    layer_out = (residual.astype(jnp.float32) + down_values).astype(jnp.bfloat16)
    return (layer_out, new_latents)


def solution(mesh):
    split = ("grp", "tq", "tr")
    tokens_spec = P(split, None)
    in_specs = (
        tokens_spec,
        P(),
        P(),
        P(),
        P(),
        P(),
        P(),
        P(),
        P(),
        P(),
        P(),
        P(("tq", "tr"), "grp"),
        P(("tq", "tr"), "grp"),
        P("grp", ("tq", "tr")),
        P("grp", ("tq", "tr"), None),
        P(None, ("tq", "tr"), None),
        P(),
        P(),
        P(),
    )
    out_specs = (tokens_spec, tokens_spec)

    def run(*args):
        n_grp, n_tok = mesh.shape["grp"], mesh.shape["tok"]
        tok_dev = args[0].shape[0] // (n_grp * n_tok)
        group_requests = tok_dev * n_tok // SPAN
        sub = Mesh(
            mesh.devices.reshape(n_grp, n_tok // group_requests, group_requests), split
        )
        return jax.shard_map(
            body, mesh=sub, in_specs=in_specs, out_specs=out_specs, check_vma=False
        )(*args)

    return run
```
